256 devices in a mesh: req: 32 (over z_hi, y, core), tp: 8 (over x, z_lo).
Axes of the slice: x: 4, y: 4, z: 8 (z_hi: 4, z_lo: 2; z = z_hi * 2 + z_lo), core: 2. Of those that a mesh axis runs over, the one named last changes fastest.
Arguments:
- hidden_in: bfloat16 [4096, 5120], P('req', 'tp'), may hold values from -6 to 6
- norm_gain: bfloat16 [5120], P('tp'), may hold values from 0.099609375 to 1.8984375
- q_weight: bfloat16 [5120, 3072], P(None, 'tp'), may hold values from -0.078125 to 0.078125
- q_bias: bfloat16 [3072], P('tp'), may hold values from -4 to 4
- k_weight: bfloat16 [5120, 1024], P(None, 'tp'), may hold values from -0.125 to 0.125
- k_bias: bfloat16 [1024], P('tp'), may hold values from -5 to 5
- v_weight: bfloat16 [5120, 1024], P(None, 'tp'), may hold values from -0.3125 to 0.3125
- v_bias: bfloat16 [1024], P('tp'), may hold values from -10 to 10
- o_weight: bfloat16 [3072, 5120], P('tp'), may hold values from -0.3125 to 0.3125
- prefix_kv: bfloat16 [32768, 2, 1024], P('req', None, 'tp'), as said below
- suffix_len: int32 [32], P('req'), may hold values from 18 to 128, as said below
- req_prefix: int32 [32], P('req'), may hold values from 0 to 3, as said below
- block_owner: int32 [32], replicated, may hold values from 0 to 31, each once
Outputs:
- attn_out: bfloat16 [4096, 5120], P('req', 'tp')
The draws below stay inside these ranges and needn't reach their ends.
Inputs may be any that keep to these rules, and one draw needn't show every extreme that they name: `suffix_len`: suffix tokens of each request; some request has exactly 128 and some exactly 18. `req_prefix`: every prefix is continued by exactly 8 requests. Block j of prefix p is held by req index block_owner[p * 8 + j]; each req index holds one block. `prefix_kv`: cached keys already carry the rotary embedding of their prefix positions.
All inputs are finite; a program needn't handle non-finite values.
Results may differ from the reference program's by a relative error of at most 0.022.
Values may be sent and summed in bfloat16 or wider, within the bound.
No kernel may reach another device: no remote copies, remote signals or barrier semaphores. Data moves between devices by JAX's collectives and lax.ppermute only.
A program may use at most 128 MiB of HBM per device.

```python
import jax
import jax.numpy as jnp
from jax import lax

D = 5120
HD = 128
KVH = 8
QH = 24
NPREF = 4
SUF = 128
PBLK = 1024
REQS = 32
OWN = 8
PREF = 8192
N_TP = 8


def draw_prefix_kv(key, part):
    key_keys, key_values = jax.random.split(jax.random.fold_in(key, 11), 2)
    rows = REQS * PBLK
    width = KVH * HD
    keys = jax.random.normal(key_keys, (rows, width), jnp.float32) * 1.5
    values = jax.random.normal(key_values, (rows, width), jnp.float32) * 4.0
    return jnp.stack([keys, values], axis=1).astype(jnp.bfloat16)


def draw_suffix_len(key, part):
    key_draw, key_rank = jax.random.split(jax.random.fold_in(key, 23))
    shortest = max(1, SUF // 7)
    lengths = jax.random.randint(key_draw, (REQS,), shortest, SUF + 1)
    ranking = jax.random.permutation(key_rank, REQS)
    lengths = lengths.at[ranking[0]].set(SUF)
    lengths = lengths.at[ranking[1]].set(shortest)
    return lengths.astype(jnp.int32)


def draw_req_prefix(key, part):
    shuffled = jax.random.permutation(jax.random.fold_in(key, 37), REQS)
    return (shuffled % NPREF).astype(jnp.int32)


def levels(rng, extent, cuts, least, largest):
    loudness, own = 1.0, jax.random.fold_in(rng, 6)
    for position, shards_of in cuts:
        draws = jnp.exp(jax.random.uniform(jax.random.fold_in(own, position), (shards_of,), jnp.float32, least / len(cuts), largest / len(cuts)))
        loudness = loudness * jnp.repeat(draws, extent[position] // shards_of).reshape([-1 if axis == position else 1 for axis in range(len(extent))])
    return loudness


def centred(rng, shape, scale, limit, shards=(), held_as=jnp.bfloat16):
    factor_of = levels(rng, shape, shards, -0.22, 0.18) if shards else 1.0
    drawn = jax.random.normal(rng, shape, jnp.float32) * scale * factor_of
    return jnp.minimum(jnp.maximum(drawn, -limit), limit).astype(held_as)


def setup_inputs(seed: int = 0) -> dict:
    splits = jax.random.split(jax.random.key(seed), 14)
    hidden_in = centred(splits[0], (REQS * SUF, D), 1.0, 6.0, ((0, 32), (1, 8)))
    norm_gain = jnp.clip(1.0 + 0.18 * jax.random.normal(splits[1], (D,), jnp.float32), 0.099609375, 1.8984375).astype(jnp.bfloat16)
    q_weight = centred(splits[2], (D, QH * HD), D ** -0.5, 0.078125, ((1, 8),))
    q_bias = centred(splits[3], (QH * HD,), 0.5, 4.0, ((0, 8),))
    k_weight = centred(splits[4], (D, KVH * HD), (D // 2) ** -0.5, 0.125, ((1, 8),))
    k_bias = centred(splits[5], (KVH * HD,), 1.0, 5.0, ((0, 8),))
    v_weight = centred(splits[6], (D, KVH * HD), (D // 16) ** -0.5, 0.3125, ((1, 8),))
    v_bias = centred(splits[7], (KVH * HD,), 2.0, 10.0, ((0, 8),))
    o_weight = centred(splits[8], (QH * HD, D), (QH * HD // 9) ** -0.5, 0.3125, ((0, 8),))
    prefix_kv = draw_prefix_kv(jax.random.fold_in(splits[13], 71), 0)
    suffix_len = draw_suffix_len(jax.random.fold_in(splits[13], 71), 0)
    req_prefix = draw_req_prefix(jax.random.fold_in(splits[13], 71), 0)
    block_owner = jax.random.permutation(splits[12], REQS).astype(jnp.int32)
    return dict(hidden_in=hidden_in, norm_gain=norm_gain, q_weight=q_weight, q_bias=q_bias, k_weight=k_weight, k_bias=k_bias, v_weight=v_weight, v_bias=v_bias, o_weight=o_weight, prefix_kv=prefix_kv, suffix_len=suffix_len, req_prefix=req_prefix, block_owner=block_owner)


THETA = 1000000.0
EPSILON = 1e-06

def rotate(heads, positions):
    half = HD // 2
    freqs = THETA ** (-(jnp.arange(half, dtype=jnp.float32) * 2.0) / HD)
    angles = positions.astype(jnp.float32)[:, None] * freqs[None, :]
    cosine = jnp.cos(angles)[:, None, :]
    sine = jnp.sin(angles)[:, None, :]
    first = heads[..., :half]
    second = heads[..., half:]
    return jnp.concatenate([first * cosine - second * sine, second * cosine + first * sine], axis=-1)

def reference(hidden_in, norm_gain, q_weight, q_bias, k_weight, k_bias, v_weight, v_bias, o_weight, prefix_kv, suffix_len, req_prefix, block_owner):
    group = QH // KVH
    tokens = hidden_in.astype(jnp.float32)
    meansq = lax.optimization_barrier(jnp.mean(tokens * tokens, axis=-1, keepdims=True))
    normed = (tokens * lax.rsqrt(meansq + EPSILON) * norm_gain.astype(jnp.float32)).astype(jnp.bfloat16)
    positions = PREF + jnp.arange(SUF, dtype=jnp.int32)
    queries = jnp.dot(normed, q_weight, preferred_element_type=jnp.float32) + q_bias.astype(jnp.float32)
    queries = rotate(queries.reshape(REQS, SUF, QH, HD), positions).astype(jnp.bfloat16)
    keys = jnp.dot(normed, k_weight, preferred_element_type=jnp.float32) + k_bias.astype(jnp.float32)
    keys = rotate(keys.reshape(REQS, SUF, KVH, HD), positions).astype(jnp.bfloat16)
    values = jnp.dot(normed, v_weight, preferred_element_type=jnp.float32) + v_bias.astype(jnp.float32)
    values = values.astype(jnp.bfloat16).reshape(REQS, SUF, KVH, HD)
    blocks = prefix_kv.reshape(REQS, PBLK, 2, KVH * HD)
    slot_index = jnp.arange(SUF, dtype=jnp.int32)
    key_index = jnp.arange(PREF + SUF, dtype=jnp.int32)
    allowed = key_index[None, :] <= (PREF + slot_index)[:, None]

    def one_request(items):
        query, key_suffix, value_suffix, which = items
        owners = lax.dynamic_slice_in_dim(block_owner, (which * OWN).astype(jnp.int32), OWN)
        cached = jnp.take(blocks, owners, axis=0).reshape(PREF, 2, KVH, HD)
        all_keys = jnp.concatenate([cached[:, 0], key_suffix], axis=0)
        all_values = jnp.concatenate([cached[:, 1], value_suffix], axis=0)
        grouped = query.reshape(SUF, KVH, group, HD)
        scores = jnp.einsum('sghd,kgd->sghk', grouped.astype(jnp.float32), all_keys.astype(jnp.float32)) * HD ** (-0.5)
        scores = jnp.where(allowed[:, None, None, :], scores, -jnp.inf)
        peak = lax.optimization_barrier(jnp.max(scores, axis=-1, keepdims=True))
        weights = jnp.exp(scores - peak)
        total = lax.optimization_barrier(jnp.sum(weights, axis=-1))
        mixed = jnp.einsum('sghk,kgd->sghd', weights.astype(jnp.bfloat16).astype(jnp.float32), all_values.astype(jnp.float32))
        context = mixed / total[..., None]
        return context.astype(jnp.bfloat16).reshape(SUF, QH * HD)
    context = lax.map(one_request, (queries, keys, values, req_prefix))
    context = context.reshape(REQS * SUF, QH * HD)
    width = QH * HD // N_TP
    pieces = context.reshape(REQS * SUF, N_TP, width).transpose(1, 0, 2)
    weights_grouped = o_weight.reshape(N_TP, width, D)

    def add_group(total, items):
        piece, weight = items
        partial_value = jnp.dot(piece, weight, preferred_element_type=jnp.float32).astype(jnp.bfloat16)
        partial_value = lax.optimization_barrier(partial_value)
        return (total + partial_value.astype(jnp.float32), None)
    summed, unused = lax.scan(add_group, jnp.zeros((REQS * SUF, D), jnp.float32), (pieces, weights_grouped))
    valid = (slot_index[None, :] < suffix_len[:, None]).reshape(REQS * SUF)
    return jnp.where(valid[:, None], summed, jnp.float32(0.0)).astype(jnp.bfloat16)
```

```python
import jax
import jax.numpy as jnp
from jax import lax
from jax.sharding import PartitionSpec as P

HD = 128
NPREF = 4


THETA = 1000000.0
EPSILON = 1e-06
ROWS = 144


def rotate(heads, positions):
    half = HD // 2
    freqs = THETA ** (-(jnp.arange(half, dtype=jnp.float32) * 2.0) / HD)
    angles = positions.astype(jnp.float32)[:, None] * freqs[None, :]
    cosine = jnp.cos(angles)[:, None, :]
    sine = jnp.sin(angles)[:, None, :]
    first = heads[..., :half]
    second = heads[..., half:]
    return jnp.concatenate(
        [first * cosine - second * sine, second * cosine + first * sine], axis=-1
    )


def split16(x):
    high = x.astype(jnp.bfloat16)
    low = (x - high.astype(jnp.float32)).astype(jnp.bfloat16)
    return high, low


def join16(high, low):
    return high.astype(jnp.float32) + low.astype(jnp.float32)


def shards(
    hidden_in,
    norm_gain,
    q_weight,
    q_bias,
    k_weight,
    k_bias,
    v_weight,
    v_bias,
    o_weight,
    prefix_kv,
    suffix_len,
    req_prefix,
    block_owner,
):
    length = hidden_in.shape[0]
    devices = lax.axis_size("req")
    owned = devices // NPREF
    block = prefix_kv.shape[0]
    prefix_len = block * owned
    kv_heads = k_weight.shape[1] // HD
    q_heads = q_weight.shape[1] // HD
    group = q_heads // kv_heads
    width = q_heads * HD
    scale = HD ** (-0.5)

    feat = hidden_in.shape[1]
    packed = jnp.concatenate(
        [hidden_in, norm_gain[None, :], jnp.zeros((ROWS - length - 1, feat), hidden_in.dtype)],
        axis=0,
    )
    full = lax.all_gather(packed, "tp", axis=1, tiled=True)
    tokens = full[:length].astype(jnp.float32)
    gain = full[length]
    meansq = jnp.mean(tokens * tokens, axis=-1, keepdims=True)
    normed = (tokens * lax.rsqrt(meansq + EPSILON) * gain.astype(jnp.float32)).astype(jnp.bfloat16)
    positions = prefix_len + jnp.arange(length, dtype=jnp.int32)
    queries = jnp.dot(normed, q_weight, preferred_element_type=jnp.float32) + q_bias.astype(
        jnp.float32
    )
    queries = rotate(queries.reshape(length, q_heads, HD), positions).astype(jnp.bfloat16)
    keys = jnp.dot(normed, k_weight, preferred_element_type=jnp.float32) + k_bias.astype(
        jnp.float32
    )
    keys = rotate(keys.reshape(length, kv_heads, HD), positions).astype(jnp.bfloat16)
    values = jnp.dot(normed, v_weight, preferred_element_type=jnp.float32) + v_bias.astype(
        jnp.float32
    )
    values = values.astype(jnp.bfloat16).reshape(length, kv_heads, HD)

    flat_q = queries.reshape(length, width)
    tag = jnp.full((1, width), req_prefix[0], jnp.int32).astype(jnp.bfloat16)
    qpack = jnp.concatenate(
        [flat_q, tag, jnp.zeros((ROWS - length - 1, width), jnp.bfloat16)], axis=0
    )
    qall = lax.all_gather(qpack, "req", axis=0, tiled=False)
    prefix_of = qall[:, length, 0].astype(jnp.int32)

    me = lax.axis_index("req")
    slots = jnp.arange(devices, dtype=jnp.int32)
    my_block = jnp.sum(jnp.where(block_owner == me, slots, 0))
    my_prefix = my_block // owned
    mine = prefix_of == my_prefix
    rank = jnp.cumsum(mine.astype(jnp.int32)) - 1
    picks = jnp.arange(owned, dtype=jnp.int32)
    chosen = jnp.sum(
        jnp.where(mine[None, :] & (rank[None, :] == picks[:, None]), slots[None, :], 0), axis=1
    )
    qsel = jnp.take(qall[:, :length], chosen, axis=0).reshape(owned, length, q_heads, HD)

    cached_k = prefix_kv[:, 0].reshape(block, HD)
    cached_v = prefix_kv[:, 1].reshape(block, HD)
    scores = jnp.einsum(
        "rshd,kd->rshk", qsel, cached_k, preferred_element_type=jnp.float32
    ) * scale
    peak = jnp.max(scores, axis=-1)
    weights = jnp.exp(scores - peak[..., None])
    total = jnp.sum(weights, axis=-1)
    mixed = jnp.einsum(
        "rshk,kd->rshd", weights.astype(jnp.bfloat16), cached_v, preferred_element_type=jnp.float32
    )
    peak_hi, peak_lo = split16(peak.reshape(owned, 1, width))
    total_hi, total_lo = split16(total.reshape(owned, 1, width))
    chunk = jnp.concatenate(
        [
            mixed.reshape(owned, length, width).astype(jnp.bfloat16),
            peak_hi,
            peak_lo,
            total_hi,
            total_lo,
            jnp.zeros((owned, ROWS - length - 4, width), jnp.bfloat16),
        ],
        axis=1,
    )
    outgoing = jnp.zeros((devices, ROWS, width), jnp.bfloat16).at[chosen].set(chunk)
    incoming = lax.all_to_all(outgoing, "req", 0, 0, tiled=True)

    slot_index = jnp.arange(length, dtype=jnp.int32)
    causal = slot_index[None, :] <= slot_index[:, None]
    grouped = queries.reshape(length, kv_heads, group, HD)
    own_scores = jnp.einsum(
        "sghd,kgd->sghk", grouped, keys, preferred_element_type=jnp.float32
    ) * scale
    own_scores = jnp.where(causal[:, None, None, :], own_scores, -jnp.inf)
    own_peak = jnp.max(own_scores, axis=-1).reshape(length, width // HD)
    own_weights = jnp.exp(own_scores - jnp.max(own_scores, axis=-1)[..., None])
    own_total = jnp.sum(own_weights, axis=-1).reshape(length, width // HD)
    own_mixed = jnp.einsum(
        "sghk,kgd->sghd", own_weights.astype(jnp.bfloat16), values, preferred_element_type=jnp.float32
    ).reshape(length, width // HD, HD)

    owners = lax.dynamic_slice_in_dim(block_owner, req_prefix[0] * owned, owned)
    got = jnp.take(incoming, owners, axis=0)
    got_mixed = got[:, :length].astype(jnp.float32).reshape(owned, length, width // HD, HD)
    got_peak = join16(got[:, length], got[:, length + 1]).reshape(owned, length, width // HD)
    got_total = join16(got[:, length + 2], got[:, length + 3]).reshape(owned, length, width // HD)
    best = jnp.maximum(own_peak, jnp.max(got_peak, axis=0))
    own_scale = jnp.exp(own_peak - best)
    got_scale = jnp.exp(got_peak - best[None])
    summed_total = own_total * own_scale + jnp.sum(got_total * got_scale, axis=0)
    summed_mixed = own_mixed * own_scale[..., None] + jnp.sum(
        got_mixed * got_scale[..., None], axis=0
    )
    context = (summed_mixed / summed_total[..., None]).astype(jnp.bfloat16).reshape(length, width)
    partial_value = jnp.dot(context, o_weight, preferred_element_type=jnp.float32)
    summed = lax.psum_scatter(
        partial_value.astype(jnp.bfloat16), "tp", scatter_dimension=1, tiled=True
    ).astype(jnp.float32)
    valid = slot_index < suffix_len[0]
    return jnp.where(valid[:, None], summed, jnp.float32(0.0)).astype(jnp.bfloat16)


def solution(mesh):
    placed = (
        P("req", "tp"),
        P("tp"),
        P(None, "tp"),
        P("tp"),
        P(None, "tp"),
        P("tp"),
        P(None, "tp"),
        P("tp"),
        P("tp", None),
        P("req", None, "tp"),
        P("req"),
        P("req"),
        P(),
    )
    return jax.shard_map(
        shards, mesh=mesh, in_specs=placed, out_specs=P("req", "tp"), check_vma=False
    )
```

```python
import jax
import jax.numpy as jnp
from jax import lax
from jax.sharding import PartitionSpec as P

HD = 128
NPREF = 4


THETA = 1000000.0
EPSILON = 1e-06
ROWS = 144


def rotate(heads, positions):
    half = HD // 2
    freqs = THETA ** (-(jnp.arange(half, dtype=jnp.float32) * 2.0) / HD)
    angles = positions.astype(jnp.float32)[:, None] * freqs[None, :]
    cosine = jnp.cos(angles)[:, None, :]
    sine = jnp.sin(angles)[:, None, :]
    first = heads[..., :half]
    second = heads[..., half:]
    return jnp.concatenate(
        [first * cosine - second * sine, second * cosine + first * sine], axis=-1
    )


def split16(x):
    high = lax.reduce_precision(x, exponent_bits=8, mantissa_bits=7)
    low = x - high
    return high.astype(jnp.bfloat16), low.astype(jnp.bfloat16)


def join16(high, low):
    return high.astype(jnp.float32) + low.astype(jnp.float32)


def shifted(x, axis, n, shift):
    return lax.ppermute(x, axis, [(i, (i + shift) % n) for i in range(n)])


def gather_by_shift(x, axis, n):
    return jnp.stack([x] + [shifted(x, axis, n, s) for s in range(1, n)])


def exchange_by_shift(x, axis, n):
    return jnp.stack([x[0]] + [shifted(x[s], axis, n, s) for s in range(1, n)])


def shards(
    hidden_in,
    norm_gain,
    q_weight,
    q_bias,
    k_weight,
    k_bias,
    v_weight,
    v_bias,
    o_weight,
    prefix_kv,
    suffix_len,
    req_prefix,
    block_owner,
):
    length = hidden_in.shape[0]
    devices = lax.axis_size("req")
    owned = devices // NPREF
    block = prefix_kv.shape[0]
    prefix_len = block * owned
    kv_heads = k_weight.shape[1] // HD
    q_heads = q_weight.shape[1] // HD
    group = q_heads // kv_heads
    width = q_heads * HD
    scale = HD ** (-0.5)

    feat = hidden_in.shape[1]
    packed = jnp.concatenate(
        [hidden_in, norm_gain[None, :], jnp.zeros((ROWS - length - 1, feat), hidden_in.dtype)],
        axis=0,
    )
    n_tp = lax.axis_size("tp")
    me_tp = lax.axis_index("tp")
    by_shift = gather_by_shift(packed, "tp", n_tp)
    ordered = jnp.take(by_shift, (me_tp - jnp.arange(n_tp, dtype=jnp.int32)) % n_tp, axis=0)
    full = ordered.transpose(1, 0, 2).reshape(ROWS, n_tp * feat)
    tokens = full[:length].astype(jnp.float32)
    gain = full[length]
    meansq = jnp.mean(tokens * tokens, axis=-1, keepdims=True)
    normed = (tokens * lax.rsqrt(meansq + EPSILON) * gain.astype(jnp.float32)).astype(jnp.bfloat16)
    positions = prefix_len + jnp.arange(length, dtype=jnp.int32)
    queries = jnp.dot(normed, q_weight, preferred_element_type=jnp.float32) + q_bias.astype(
        jnp.float32
    )
    queries = rotate(queries.reshape(length, q_heads, HD), positions).astype(jnp.bfloat16)
    keys = jnp.dot(normed, k_weight, preferred_element_type=jnp.float32) + k_bias.astype(
        jnp.float32
    )
    keys = rotate(keys.reshape(length, kv_heads, HD), positions).astype(jnp.bfloat16)
    values = jnp.dot(normed, v_weight, preferred_element_type=jnp.float32) + v_bias.astype(
        jnp.float32
    )
    values = values.astype(jnp.bfloat16).reshape(length, kv_heads, HD)

    flat_q = queries.reshape(length, width)
    tag = jnp.full((1, width), req_prefix[0], jnp.int32).astype(jnp.bfloat16)
    qpack = jnp.concatenate(
        [flat_q, tag, jnp.zeros((ROWS - length - 1, width), jnp.bfloat16)], axis=0
    )
    qall = gather_by_shift(qpack, "req", devices)
    me = lax.axis_index("req")
    slots = jnp.arange(devices, dtype=jnp.int32)
    prefix_of = jnp.take(qall[:, length, 0].astype(jnp.int32), (me - slots) % devices)
    my_block = jnp.sum(jnp.where(block_owner == me, slots, 0))
    my_prefix = my_block // owned
    mine = prefix_of == my_prefix
    rank = jnp.cumsum(mine.astype(jnp.int32)) - 1
    picks = jnp.arange(owned, dtype=jnp.int32)
    chosen = jnp.sum(
        jnp.where(mine[None, :] & (rank[None, :] == picks[:, None]), slots[None, :], 0), axis=1
    )
    qsel = jnp.take(qall[:, :length], (me - chosen) % devices, axis=0).reshape(owned, length, q_heads, HD)

    cached_k = prefix_kv[:, 0].reshape(block, HD)
    cached_v = prefix_kv[:, 1].reshape(block, HD)
    scores = jnp.einsum(
        "rshd,kd->rshk", qsel, cached_k, preferred_element_type=jnp.float32
    ) * scale
    peak = jnp.max(scores, axis=-1)
    weights = jnp.exp(scores - peak[..., None])
    total = jnp.sum(weights, axis=-1)
    mixed = jnp.einsum(
        "rshk,kd->rshd", weights.astype(jnp.bfloat16), cached_v, preferred_element_type=jnp.float32
    )
    peak_hi, peak_lo = split16(peak.reshape(owned, 1, width))
    total_hi, total_lo = split16(total.reshape(owned, 1, width))
    chunk = jnp.concatenate(
        [
            mixed.reshape(owned, length, width).astype(jnp.bfloat16),
            peak_hi,
            peak_lo,
            total_hi,
            total_lo,
            jnp.zeros((owned, ROWS - length - 4, width), jnp.bfloat16),
        ],
        axis=1,
    )
    outgoing = jnp.zeros((devices, ROWS, width), jnp.bfloat16).at[(chosen - me) % devices].set(chunk)
    incoming = exchange_by_shift(outgoing, "req", devices)

    slot_index = jnp.arange(length, dtype=jnp.int32)
    causal = slot_index[None, :] <= slot_index[:, None]
    grouped = queries.reshape(length, kv_heads, group, HD)
    own_scores = jnp.einsum(
        "sghd,kgd->sghk", grouped, keys, preferred_element_type=jnp.float32
    ) * scale
    own_scores = jnp.where(causal[:, None, None, :], own_scores, -jnp.inf)
    own_peak = jnp.max(own_scores, axis=-1).reshape(length, width // HD)
    own_weights = jnp.exp(own_scores - jnp.max(own_scores, axis=-1)[..., None])
    own_total = jnp.sum(own_weights, axis=-1).reshape(length, width // HD)
    own_mixed = jnp.einsum(
        "sghk,kgd->sghd", own_weights.astype(jnp.bfloat16), values, preferred_element_type=jnp.float32
    ).reshape(length, width // HD, HD)

    owners = lax.dynamic_slice_in_dim(block_owner, req_prefix[0] * owned, owned)
    got = jnp.take(incoming, (me - owners) % devices, axis=0)
    got_mixed = got[:, :length].astype(jnp.float32).reshape(owned, length, width // HD, HD)
    got_peak = join16(got[:, length], got[:, length + 1]).reshape(owned, length, width // HD)
    got_total = join16(got[:, length + 2], got[:, length + 3]).reshape(owned, length, width // HD)
    best = jnp.maximum(own_peak, jnp.max(got_peak, axis=0))
    own_scale = jnp.exp(own_peak - best)
    got_scale = jnp.exp(got_peak - best[None])
    summed_total = own_total * own_scale + jnp.sum(got_total * got_scale, axis=0)
    summed_mixed = own_mixed * own_scale[..., None] + jnp.sum(
        got_mixed * got_scale[..., None], axis=0
    )
    context = (summed_mixed / summed_total[..., None]).astype(jnp.bfloat16).reshape(length, width)
    partial_value = jnp.dot(context, o_weight, preferred_element_type=jnp.float32)
    pieces = partial_value.astype(jnp.bfloat16).reshape(length, n_tp, feat).transpose(1, 0, 2)
    pieces = jnp.take(pieces, (me_tp + jnp.arange(n_tp, dtype=jnp.int32)) % n_tp, axis=0)
    summed = jnp.sum(exchange_by_shift(pieces, "tp", n_tp).astype(jnp.float32), axis=0)
    valid = slot_index < suffix_len[0]
    return jnp.where(valid[:, None], summed, jnp.float32(0.0)).astype(jnp.bfloat16)


def solution(mesh):
    placed = (
        P("req", "tp"),
        P("tp"),
        P(None, "tp"),
        P("tp"),
        P(None, "tp"),
        P("tp"),
        P(None, "tp"),
        P("tp"),
        P("tp", None),
        P("req", None, "tp"),
        P("req"),
        P("req"),
        P(),
    )
    return jax.shard_map(
        shards, mesh=mesh, in_specs=placed, out_specs=P("req", "tp"), check_vma=False
    )
```

```python
import jax
import jax.numpy as jnp
from jax import lax
from jax.sharding import PartitionSpec as P

HD = 128
NPREF = 4


THETA = 1000000.0
EPSILON = 1e-06
ROWS = 144


def rotate(heads, positions):
    half = HD // 2
    freqs = THETA ** (-(jnp.arange(half, dtype=jnp.float32) * 2.0) / HD)
    angles = positions.astype(jnp.float32)[:, None] * freqs[None, :]
    cosine = jnp.cos(angles)[:, None, :]
    sine = jnp.sin(angles)[:, None, :]
    first = heads[..., :half]
    second = heads[..., half:]
    return jnp.concatenate(
        [first * cosine - second * sine, second * cosine + first * sine], axis=-1
    )


def block_stats(grouped, keys, values, allowed):
    scores = jnp.einsum(
        "sghd,kgd->sghk", grouped, keys, preferred_element_type=jnp.float32
    ) * HD ** (-0.5)
    if allowed is not None:
        scores = jnp.where(allowed[:, None, None, :], scores, -jnp.inf)
    peak = jnp.max(scores, axis=-1)
    weights = jnp.exp(scores - peak[..., None])
    total = jnp.sum(weights, axis=-1)
    mixed = jnp.einsum(
        "sghk,kgd->sghd", weights.astype(jnp.bfloat16), values, preferred_element_type=jnp.float32
    )
    return (peak, total, mixed)


def combine(first, second):
    peak = jnp.maximum(first[0], second[0])
    left = jnp.exp(first[0] - peak)
    right = jnp.exp(second[0] - peak)
    total = first[1] * left + second[1] * right
    mixed = first[2] * left[..., None] + second[2] * right[..., None]
    return (peak, total, mixed)


def shards(
    hidden_in,
    norm_gain,
    q_weight,
    q_bias,
    k_weight,
    k_bias,
    v_weight,
    v_bias,
    o_weight,
    prefix_kv,
    suffix_len,
    req_prefix,
    block_owner,
):
    length = hidden_in.shape[0]
    devices = lax.axis_size("req")
    owned = devices // NPREF
    block = prefix_kv.shape[0]
    prefix_len = block * owned
    kv_heads = k_weight.shape[1] // HD
    q_heads = q_weight.shape[1] // HD
    group = q_heads // kv_heads
    feat = hidden_in.shape[1]
    n_tp = lax.axis_size("tp")
    packed = jnp.concatenate(
        [hidden_in, norm_gain[None, :], jnp.zeros((ROWS - length - 1, feat), hidden_in.dtype)],
        axis=0,
    )
    spread = jnp.broadcast_to(packed[None], (n_tp,) + packed.shape)
    pieces_in = lax.all_to_all(spread, "tp", 0, 0, tiled=True)
    full = pieces_in.transpose(1, 0, 2).reshape(ROWS, n_tp * feat)
    tokens = full[:length].astype(jnp.float32)
    gain = full[length]
    meansq = jnp.mean(tokens * tokens, axis=-1, keepdims=True)
    normed = (tokens * lax.rsqrt(meansq + EPSILON) * gain.astype(jnp.float32)).astype(jnp.bfloat16)
    positions = prefix_len + jnp.arange(length, dtype=jnp.int32)
    queries = jnp.dot(normed, q_weight, preferred_element_type=jnp.float32) + q_bias.astype(
        jnp.float32
    )
    queries = rotate(queries.reshape(length, q_heads, HD), positions).astype(jnp.bfloat16)
    queries = queries.reshape(length, kv_heads, group, HD)
    keys = jnp.dot(normed, k_weight, preferred_element_type=jnp.float32) + k_bias.astype(
        jnp.float32
    )
    keys = rotate(keys.reshape(length, kv_heads, HD), positions).astype(jnp.bfloat16)
    values = jnp.dot(normed, v_weight, preferred_element_type=jnp.float32) + v_bias.astype(
        jnp.float32
    )
    values = values.astype(jnp.bfloat16).reshape(length, kv_heads, HD)
    slot_index = jnp.arange(length, dtype=jnp.int32)
    causal = slot_index[None, :] <= slot_index[:, None]
    state = block_stats(queries, keys, values, causal)
    which = req_prefix[0]

    def advance(current, cached):
        return (combine(current, block_stats(queries, cached[:, 0], cached[:, 1], None)), None)

    everything = lax.all_gather(prefix_kv, "req", axis=0, tiled=True)
    stacked = everything.reshape(devices, block, 2, kv_heads, HD)
    owners = lax.dynamic_slice_in_dim(block_owner, which * owned, owned)
    chosen = jnp.take(stacked, owners, axis=0)
    state, unused = lax.scan(advance, state, chosen)
    peak, total, mixed = state
    context = (mixed / total[..., None]).astype(jnp.bfloat16).reshape(length, q_heads * HD)
    partial_value = jnp.dot(context, o_weight, preferred_element_type=jnp.float32)
    pieces_out = partial_value.astype(jnp.bfloat16).reshape(length, n_tp, feat).transpose(1, 0, 2)
    summed = jnp.sum(lax.all_to_all(pieces_out, "tp", 0, 0, tiled=True).astype(jnp.float32), axis=0)
    valid = slot_index < suffix_len[0]
    return jnp.where(valid[:, None], summed, jnp.float32(0.0)).astype(jnp.bfloat16)


def solution(mesh):
    placed = (
        P("req", "tp"),
        P("tp"),
        P(None, "tp"),
        P("tp"),
        P(None, "tp"),
        P("tp"),
        P(None, "tp"),
        P("tp"),
        P("tp", None),
        P("req", None, "tp"),
        P("req"),
        P("req"),
        P(),
    )
    return jax.shard_map(
        shards, mesh=mesh, in_specs=placed, out_specs=P("req", "tp"), check_vma=False
    )
```

```python
import jax
import jax.numpy as jnp
from jax import lax
from jax.experimental import pallas as pl
from jax.experimental.pallas import tpu as pltpu
from jax.sharding import PartitionSpec as P

HD = 128
NPREF = 4


THETA = 1000000.0
EPSILON = 1e-06
ROWS = 144


def rotate(heads, positions):
    half = HD // 2
    freqs = THETA ** (-(jnp.arange(half, dtype=jnp.float32) * 2.0) / HD)
    angles = positions.astype(jnp.float32)[:, None] * freqs[None, :]
    cosine = jnp.cos(angles)[:, None, :]
    sine = jnp.sin(angles)[:, None, :]
    first = heads[..., :half]
    second = heads[..., half:]
    return jnp.concatenate(
        [first * cosine - second * sine, second * cosine + first * sine], axis=-1
    )


def block_stats(grouped, keys, values, allowed):
    scores = jnp.einsum(
        "sghd,kgd->sghk", grouped, keys, preferred_element_type=jnp.float32
    ) * HD ** (-0.5)
    if allowed is not None:
        scores = jnp.where(allowed[:, None, None, :], scores, -jnp.inf)
    peak = jnp.max(scores, axis=-1)
    weights = jnp.exp(scores - peak[..., None])
    total = jnp.sum(weights, axis=-1)
    mixed = jnp.einsum(
        "sghk,kgd->sghd", weights.astype(jnp.bfloat16), values, preferred_element_type=jnp.float32
    )
    return (peak, total, mixed)


def combine(first, second):
    peak = jnp.maximum(first[0], second[0])
    left = jnp.exp(first[0] - peak)
    right = jnp.exp(second[0] - peak)
    total = first[1] * left + second[1] * right
    mixed = first[2] * left[..., None] + second[2] * right[..., None]
    return (peak, total, mixed)


def prefix_kernel(own_ref, q_ref, k_ref, v_ref, m0_ref, l0_ref, a0_ref, o_ref, m_sc, l_sc, acc_sc):
    step = pl.program_id(0)
    group = q_ref.shape[1] // HD

    @pl.when(step == 0)
    def _():
        m_sc[...] = m0_ref[...]
        l_sc[...] = l0_ref[...]
        acc_sc[...] = a0_ref[...]

    q = q_ref[...]
    stacked = jnp.concatenate([q[:, h * HD:(h + 1) * HD] for h in range(group)], axis=0)
    keys = k_ref[0]
    values = v_ref[0]
    scores = lax.dot_general(
        stacked, keys, (((1,), (1,)), ((), ())), preferred_element_type=jnp.float32
    ) * HD ** (-0.5)
    old = m_sc[...]
    new = jnp.maximum(old, jnp.max(scores, axis=-1, keepdims=True))
    alpha = jnp.exp(old - new)
    weights = jnp.exp(scores - new)
    l_sc[...] = alpha * l_sc[...] + jnp.sum(weights, axis=-1, keepdims=True)
    acc_sc[...] = alpha * acc_sc[...] + jnp.dot(
        weights.astype(jnp.bfloat16), values, preferred_element_type=jnp.float32
    )
    m_sc[...] = new

    @pl.when(step == pl.num_programs(0) - 1)
    def _():
        context = acc_sc[...] / l_sc[...]
        rows = q_ref.shape[0]
        for h in range(group):
            o_ref[:, h * HD:(h + 1) * HD] = context[h * rows:(h + 1) * rows].astype(o_ref.dtype)


def prefix_attention(owners, flat_q, kv, peak0, total0, mixed0):
    length, width = flat_q.shape
    steps = owners.shape[0]
    block = kv.shape[1]
    rows = peak0.shape[0]
    cost = pl.CostEstimate(
        flops=4 * rows * block * HD * steps,
        transcendentals=rows * block * steps,
        bytes_accessed=2 * steps * block * HD * 2 + length * width * 4 + rows * HD * 4,
    )
    return pl.pallas_call(
        prefix_kernel,
        out_shape=jax.ShapeDtypeStruct((length, width), jnp.bfloat16),
        grid_spec=pltpu.PrefetchScalarGridSpec(
            num_scalar_prefetch=1,
            grid=(steps,),
            in_specs=[
                pl.BlockSpec((length, width), lambda j, own: (0, 0)),
                pl.BlockSpec((1, block, HD), lambda j, own: (own[j], 0, 0)),
                pl.BlockSpec((1, block, HD), lambda j, own: (own[j], 0, 1)),
                pl.BlockSpec((rows, 1), lambda j, own: (0, 0)),
                pl.BlockSpec((rows, 1), lambda j, own: (0, 0)),
                pl.BlockSpec((rows, HD), lambda j, own: (0, 0)),
            ],
            out_specs=pl.BlockSpec((length, width), lambda j, own: (0, 0)),
            scratch_shapes=[
                pltpu.VMEM((rows, 1), jnp.float32),
                pltpu.VMEM((rows, 1), jnp.float32),
                pltpu.VMEM((rows, HD), jnp.float32),
            ],
        ),
        compiler_params=pltpu.CompilerParams(dimension_semantics=("arbitrary",)),
        cost_estimate=cost,
    )(owners, flat_q, kv, kv, peak0, total0, mixed0)


def shards(
    hidden_in,
    norm_gain,
    q_weight,
    q_bias,
    k_weight,
    k_bias,
    v_weight,
    v_bias,
    o_weight,
    prefix_kv,
    suffix_len,
    req_prefix,
    block_owner,
):
    length = hidden_in.shape[0]
    devices = lax.axis_size("req")
    owned = devices // NPREF
    block = prefix_kv.shape[0]
    prefix_len = block * owned
    kv_heads = k_weight.shape[1] // HD
    q_heads = q_weight.shape[1] // HD
    group = q_heads // kv_heads
    feat = hidden_in.shape[1]
    n_tp = lax.axis_size("tp")
    packed = jnp.concatenate(
        [hidden_in, norm_gain[None, :], jnp.zeros((ROWS - length - 1, feat), hidden_in.dtype)],
        axis=0,
    )
    spread = jnp.broadcast_to(packed[None], (n_tp,) + packed.shape)
    pieces_in = lax.all_to_all(spread, "tp", 0, 0, tiled=True)
    full = pieces_in.transpose(1, 0, 2).reshape(ROWS, n_tp * feat)
    tokens = full[:length].astype(jnp.float32)
    gain = full[length]
    meansq = jnp.mean(tokens * tokens, axis=-1, keepdims=True)
    normed = (tokens * lax.rsqrt(meansq + EPSILON) * gain.astype(jnp.float32)).astype(jnp.bfloat16)
    positions = prefix_len + jnp.arange(length, dtype=jnp.int32)
    queries = jnp.dot(normed, q_weight, preferred_element_type=jnp.float32) + q_bias.astype(
        jnp.float32
    )
    queries = rotate(queries.reshape(length, q_heads, HD), positions).astype(jnp.bfloat16)
    queries = queries.reshape(length, kv_heads, group, HD)
    keys = jnp.dot(normed, k_weight, preferred_element_type=jnp.float32) + k_bias.astype(
        jnp.float32
    )
    keys = rotate(keys.reshape(length, kv_heads, HD), positions).astype(jnp.bfloat16)
    values = jnp.dot(normed, v_weight, preferred_element_type=jnp.float32) + v_bias.astype(
        jnp.float32
    )
    values = values.astype(jnp.bfloat16).reshape(length, kv_heads, HD)
    slot_index = jnp.arange(length, dtype=jnp.int32)
    causal = slot_index[None, :] <= slot_index[:, None]
    peak, total, mixed = block_stats(queries, keys, values, causal)
    rows = length * q_heads
    peak0 = peak.reshape(length, q_heads).T.reshape(rows, 1)
    total0 = total.reshape(length, q_heads).T.reshape(rows, 1)
    mixed0 = mixed.reshape(length, q_heads, HD).transpose(1, 0, 2).reshape(rows, HD)
    which = req_prefix[0]
    rowwise = prefix_kv.reshape(block, 2 * kv_heads * HD)
    gathered = lax.all_gather(rowwise, "req", axis=0, tiled=True)
    stacked = gathered.reshape(devices, block, 2 * kv_heads * HD)
    owners = lax.dynamic_slice_in_dim(block_owner, which * owned, owned)
    context = prefix_attention(
        owners, queries.reshape(length, q_heads * HD), stacked, peak0, total0, mixed0
    )
    partial_value = jnp.dot(context, o_weight, preferred_element_type=jnp.float32)
    pieces_out = partial_value.astype(jnp.bfloat16).reshape(length, n_tp, feat).transpose(1, 0, 2)
    summed = jnp.sum(lax.all_to_all(pieces_out, "tp", 0, 0, tiled=True).astype(jnp.float32), axis=0)
    valid = slot_index < suffix_len[0]
    return jnp.where(valid[:, None], summed, jnp.float32(0.0)).astype(jnp.bfloat16)


def solution(mesh):
    placed = (
        P("req", "tp"),
        P("tp"),
        P(None, "tp"),
        P("tp"),
        P(None, "tp"),
        P("tp"),
        P(None, "tp"),
        P("tp"),
        P("tp", None),
        P("req", None, "tp"),
        P("req"),
        P("req"),
        P(),
    )
    return jax.shard_map(
        shards, mesh=mesh, in_specs=placed, out_specs=P("req", "tp"), check_vma=False
    )
```

```python
import jax
import jax.numpy as jnp
from jax import lax
from jax.experimental import pallas as pl
from jax.experimental.pallas import tpu as pltpu
from jax.sharding import PartitionSpec as P

HD = 128
NPREF = 4


THETA = 1000000.0
EPSILON = 1e-06
ROWS = 144


def rotate(heads, positions):
    half = HD // 2
    freqs = THETA ** (-(jnp.arange(half, dtype=jnp.float32) * 2.0) / HD)
    angles = positions.astype(jnp.float32)[:, None] * freqs[None, :]
    cosine = jnp.cos(angles)[:, None, :]
    sine = jnp.sin(angles)[:, None, :]
    first = heads[..., :half]
    second = heads[..., half:]
    return jnp.concatenate(
        [first * cosine - second * sine, second * cosine + first * sine], axis=-1
    )


def block_stats(grouped, keys, values, allowed):
    scores = jnp.einsum(
        "sghd,kgd->sghk", grouped, keys, preferred_element_type=jnp.float32
    ) * HD ** (-0.5)
    if allowed is not None:
        scores = jnp.where(allowed[:, None, None, :], scores, -jnp.inf)
    peak = jnp.max(scores, axis=-1)
    weights = jnp.exp(scores - peak[..., None])
    total = jnp.sum(weights, axis=-1)
    mixed = jnp.einsum(
        "sghk,kgd->sghd", weights.astype(jnp.bfloat16), values, preferred_element_type=jnp.float32
    )
    return (peak, total, mixed)


def combine(first, second):
    peak = jnp.maximum(first[0], second[0])
    left = jnp.exp(first[0] - peak)
    right = jnp.exp(second[0] - peak)
    total = first[1] * left + second[1] * right
    mixed = first[2] * left[..., None] + second[2] * right[..., None]
    return (peak, total, mixed)


def prefix_kernel(
    local_ref, use_ref, q_ref, ka_ref, va_ref, kb_ref, vb_ref, m0_ref, l0_ref, a0_ref,
    o_ref, m_sc, l_sc, acc_sc,
):
    step = pl.program_id(0)
    group = q_ref.shape[1] // HD

    @pl.when(step == 0)
    def _():
        m_sc[...] = m0_ref[...]
        l_sc[...] = l0_ref[...]
        acc_sc[...] = a0_ref[...]

    q = q_ref[...]
    stacked = jnp.concatenate([q[:, h * HD:(h + 1) * HD] for h in range(group)], axis=0)
    here = use_ref[step] == 1
    keys = jnp.where(here, ka_ref[0], kb_ref[0])
    values = jnp.where(here, va_ref[0], vb_ref[0])
    scores = lax.dot_general(
        stacked, keys, (((1,), (1,)), ((), ())), preferred_element_type=jnp.float32
    ) * HD ** (-0.5)
    old = m_sc[...]
    new = jnp.maximum(old, jnp.max(scores, axis=-1, keepdims=True))
    alpha = jnp.exp(old - new)
    weights = jnp.exp(scores - new)
    l_sc[...] = alpha * l_sc[...] + jnp.sum(weights, axis=-1, keepdims=True)
    acc_sc[...] = alpha * acc_sc[...] + jnp.dot(
        weights.astype(jnp.bfloat16), values, preferred_element_type=jnp.float32
    )
    m_sc[...] = new

    @pl.when(step == pl.num_programs(0) - 1)
    def _():
        context = acc_sc[...] / l_sc[...]
        rows = q_ref.shape[0]
        for h in range(group):
            o_ref[:, h * HD:(h + 1) * HD] = context[h * rows:(h + 1) * rows].astype(o_ref.dtype)


def prefix_attention(local, use, flat_q, mine, received, peak0, total0, mixed0):
    length, width = flat_q.shape
    steps = local.shape[0]
    block = mine.shape[1]
    rows = peak0.shape[0]
    cost = pl.CostEstimate(
        flops=4 * rows * block * HD * steps,
        transcendentals=rows * block * steps,
        bytes_accessed=4 * steps * block * HD * 2 + length * width * 4 + rows * HD * 4,
    )
    return pl.pallas_call(
        prefix_kernel,
        out_shape=jax.ShapeDtypeStruct((length, width), jnp.bfloat16),
        grid_spec=pltpu.PrefetchScalarGridSpec(
            num_scalar_prefetch=2,
            grid=(steps,),
            in_specs=[
                pl.BlockSpec((length, width), lambda j, loc, use: (0, 0)),
                pl.BlockSpec((1, block, HD), lambda j, loc, use: (loc[j], 0, 0)),
                pl.BlockSpec((1, block, HD), lambda j, loc, use: (loc[j], 0, 1)),
                pl.BlockSpec((1, block, HD), lambda j, loc, use: (j, 0, 0)),
                pl.BlockSpec((1, block, HD), lambda j, loc, use: (j, 0, 1)),
                pl.BlockSpec((rows, 1), lambda j, loc, use: (0, 0)),
                pl.BlockSpec((rows, 1), lambda j, loc, use: (0, 0)),
                pl.BlockSpec((rows, HD), lambda j, loc, use: (0, 0)),
            ],
            out_specs=pl.BlockSpec((length, width), lambda j, loc, use: (0, 0)),
            scratch_shapes=[
                pltpu.VMEM((rows, 1), jnp.float32),
                pltpu.VMEM((rows, 1), jnp.float32),
                pltpu.VMEM((rows, HD), jnp.float32),
            ],
        ),
        compiler_params=pltpu.CompilerParams(dimension_semantics=("arbitrary",)),
        cost_estimate=cost,
    )(local, use, flat_q, mine, mine, received, received, peak0, total0, mixed0)


def shards(
    hidden_in,
    norm_gain,
    q_weight,
    q_bias,
    k_weight,
    k_bias,
    v_weight,
    v_bias,
    o_weight,
    prefix_kv,
    suffix_len,
    req_prefix,
    block_owner,
):
    length = hidden_in.shape[0]
    devices = lax.axis_size("req")
    owned = devices // NPREF
    block = prefix_kv.shape[0]
    prefix_len = block * owned
    kv_heads = k_weight.shape[1] // HD
    q_heads = q_weight.shape[1] // HD
    group = q_heads // kv_heads
    feat = hidden_in.shape[1]
    n_tp = lax.axis_size("tp")
    packed = jnp.concatenate(
        [hidden_in, norm_gain[None, :], jnp.zeros((ROWS - length - 1, feat), hidden_in.dtype)],
        axis=0,
    )
    spread = jnp.broadcast_to(packed[None], (n_tp,) + packed.shape)
    pieces_in = lax.all_to_all(spread, "tp", 0, 0, tiled=True)
    full = pieces_in.transpose(1, 0, 2).reshape(ROWS, n_tp * feat)
    tokens = full[:length].astype(jnp.float32)
    gain = full[length]
    meansq = jnp.mean(tokens * tokens, axis=-1, keepdims=True)
    normed = (tokens * lax.rsqrt(meansq + EPSILON) * gain.astype(jnp.float32)).astype(jnp.bfloat16)
    positions = prefix_len + jnp.arange(length, dtype=jnp.int32)
    queries = jnp.dot(normed, q_weight, preferred_element_type=jnp.float32) + q_bias.astype(
        jnp.float32
    )
    queries = rotate(queries.reshape(length, q_heads, HD), positions).astype(jnp.bfloat16)
    queries = queries.reshape(length, kv_heads, group, HD)
    keys = jnp.dot(normed, k_weight, preferred_element_type=jnp.float32) + k_bias.astype(
        jnp.float32
    )
    keys = rotate(keys.reshape(length, kv_heads, HD), positions).astype(jnp.bfloat16)
    values = jnp.dot(normed, v_weight, preferred_element_type=jnp.float32) + v_bias.astype(
        jnp.float32
    )
    values = values.astype(jnp.bfloat16).reshape(length, kv_heads, HD)
    slot_index = jnp.arange(length, dtype=jnp.int32)
    causal = slot_index[None, :] <= slot_index[:, None]
    peak, total, mixed = block_stats(queries, keys, values, causal)
    rows = length * q_heads
    peak0 = peak.reshape(length, q_heads).T.reshape(rows, 1)
    total0 = total.reshape(length, q_heads).T.reshape(rows, 1)
    mixed0 = mixed.reshape(length, q_heads, HD).transpose(1, 0, 2).reshape(rows, HD)
    which = req_prefix[0]
    me = lax.axis_index("req")
    parity = me % 2
    pairs = [(i, i ^ 1) for i in range(devices)]
    partner_prefix = lax.ppermute(req_prefix, "req", pairs)[0]
    rowwise = prefix_kv.reshape(block, 2 * kv_heads * HD)
    halves = [list(range(c, devices, 2)) for c in range(2)]
    gathered = lax.all_gather(rowwise, "req", axis=0, tiled=True, axis_index_groups=halves)
    mine = gathered.reshape(devices // 2, block, 2 * kv_heads * HD)
    wanted = lax.dynamic_slice_in_dim(block_owner, partner_prefix * owned, owned)
    offer = jnp.where(wanted % 2 == parity, wanted // 2, 0)
    received = lax.ppermute(jnp.take(mine, offer, axis=0), "req", pairs)
    owners = lax.dynamic_slice_in_dim(block_owner, which * owned, owned)
    use = (owners % 2 == parity).astype(jnp.int32)
    local = jnp.where(use == 1, owners // 2, 0)
    context = prefix_attention(
        local, use, queries.reshape(length, q_heads * HD), mine, received, peak0, total0, mixed0
    )
    partial_value = jnp.dot(context, o_weight, preferred_element_type=jnp.float32)
    pieces_out = partial_value.astype(jnp.bfloat16).reshape(length, n_tp, feat).transpose(1, 0, 2)
    summed = jnp.sum(lax.all_to_all(pieces_out, "tp", 0, 0, tiled=True).astype(jnp.float32), axis=0)
    valid = slot_index < suffix_len[0]
    return jnp.where(valid[:, None], summed, jnp.float32(0.0)).astype(jnp.bfloat16)


def solution(mesh):
    placed = (
        P("req", "tp"),
        P("tp"),
        P(None, "tp"),
        P("tp"),
        P(None, "tp"),
        P("tp"),
        P(None, "tp"),
        P("tp"),
        P("tp", None),
        P("req", None, "tp"),
        P("req"),
        P("req"),
        P(),
    )
    return jax.shard_map(
        shards, mesh=mesh, in_specs=placed, out_specs=P("req", "tp"), check_vma=False
    )
```

```python
import jax
import jax.numpy as jnp
from jax import lax
from jax.experimental import pallas as pl
from jax.experimental.pallas import tpu as pltpu
from jax.sharding import PartitionSpec as P

HD = 128
NPREF = 4


THETA = 1000000.0
EPSILON = 1e-06
ROWS = 144


def rotate(heads, positions):
    half = HD // 2
    freqs = THETA ** (-(jnp.arange(half, dtype=jnp.float32) * 2.0) / HD)
    angles = positions.astype(jnp.float32)[:, None] * freqs[None, :]
    cosine = jnp.cos(angles)[:, None, :]
    sine = jnp.sin(angles)[:, None, :]
    first = heads[..., :half]
    second = heads[..., half:]
    return jnp.concatenate(
        [first * cosine - second * sine, second * cosine + first * sine], axis=-1
    )


def block_stats(grouped, keys, values, allowed):
    scores = jnp.einsum(
        "sghd,kgd->sghk", grouped, keys, preferred_element_type=jnp.float32
    ) * HD ** (-0.5)
    if allowed is not None:
        scores = jnp.where(allowed[:, None, None, :], scores, -jnp.inf)
    peak = jnp.max(scores, axis=-1)
    weights = jnp.exp(scores - peak[..., None])
    total = jnp.sum(weights, axis=-1)
    mixed = jnp.einsum(
        "sghk,kgd->sghd", weights.astype(jnp.bfloat16), values, preferred_element_type=jnp.float32
    )
    return (peak, total, mixed)


def combine(first, second):
    peak = jnp.maximum(first[0], second[0])
    left = jnp.exp(first[0] - peak)
    right = jnp.exp(second[0] - peak)
    total = first[1] * left + second[1] * right
    mixed = first[2] * left[..., None] + second[2] * right[..., None]
    return (peak, total, mixed)


def prefix_kernel(
    own_ref, q_ref, k_ref, v_ref, m0_ref, l0_ref, a0_ref, w_hbm, o_ref, m_sc, l_sc, acc_sc, w_sc, sem
):
    step = pl.program_id(0)
    group = q_ref.shape[1] // HD
    fetch = pltpu.make_async_copy(w_hbm, w_sc, sem.at[0])

    @pl.when(step == 0)
    def _():
        fetch.start()
        m_sc[...] = m0_ref[...]
        l_sc[...] = l0_ref[...]
        acc_sc[...] = a0_ref[...]

    q = q_ref[...]
    stacked = jnp.concatenate([q[:, h * HD:(h + 1) * HD] for h in range(group)], axis=0)
    keys = k_ref[0]
    values = v_ref[0]
    scores = lax.dot_general(
        stacked, keys, (((1,), (1,)), ((), ())), preferred_element_type=jnp.float32
    ) * HD ** (-0.5)
    old = m_sc[...]
    new = jnp.maximum(old, jnp.max(scores, axis=-1, keepdims=True))
    alpha = jnp.exp(old - new)
    weights = jnp.exp(scores - new)
    l_sc[...] = alpha * l_sc[...] + jnp.sum(weights, axis=-1, keepdims=True)
    acc_sc[...] = alpha * acc_sc[...] + jnp.dot(
        weights.astype(jnp.bfloat16), values, preferred_element_type=jnp.float32
    )
    m_sc[...] = new

    @pl.when(step == pl.num_programs(0) - 1)
    def _():
        context = (acc_sc[...] / l_sc[...]).astype(jnp.bfloat16)
        rows = q_ref.shape[0]
        flat = jnp.concatenate([context[h * rows:(h + 1) * rows] for h in range(group)], axis=1)
        fetch.wait()
        partial = jnp.dot(flat, w_sc[...], preferred_element_type=jnp.float32).astype(o_ref.dtype)
        pieces = o_ref.shape[0]
        span = o_ref.shape[2]
        for t in range(pieces):
            o_ref[t] = partial[:, t * span:(t + 1) * span]


def prefix_attention(owners, flat_q, kv, peak0, total0, mixed0, o_weight, pieces):
    length, width = flat_q.shape
    out_width = o_weight.shape[1]
    steps = owners.shape[0]
    block = kv.shape[1]
    rows = peak0.shape[0]
    cost = pl.CostEstimate(
        flops=4 * rows * block * HD * steps,
        transcendentals=rows * block * steps,
        bytes_accessed=2 * steps * block * HD * 2 + length * width * 4 + rows * HD * 4
        + width * out_width * 2 + length * out_width * 2,
    )
    return pl.pallas_call(
        prefix_kernel,
        out_shape=jax.ShapeDtypeStruct((pieces, length, out_width // pieces), jnp.bfloat16),
        grid_spec=pltpu.PrefetchScalarGridSpec(
            num_scalar_prefetch=1,
            grid=(steps,),
            in_specs=[
                pl.BlockSpec((length, width), lambda j, own: (0, 0)),
                pl.BlockSpec((1, block, HD), lambda j, own: (own[j], 0, 0)),
                pl.BlockSpec((1, block, HD), lambda j, own: (own[j], 0, 1)),
                pl.BlockSpec((rows, 1), lambda j, own: (0, 0)),
                pl.BlockSpec((rows, 1), lambda j, own: (0, 0)),
                pl.BlockSpec((rows, HD), lambda j, own: (0, 0)),
                pl.BlockSpec(memory_space=pl.ANY),
            ],
            out_specs=pl.BlockSpec((pieces, length, out_width // pieces), lambda j, own: (0, 0, 0)),
            scratch_shapes=[
                pltpu.VMEM((rows, 1), jnp.float32),
                pltpu.VMEM((rows, 1), jnp.float32),
                pltpu.VMEM((rows, HD), jnp.float32),
                pltpu.VMEM((width, out_width), jnp.bfloat16),
                pltpu.SemaphoreType.DMA((1,)),
            ],
        ),
        compiler_params=pltpu.CompilerParams(dimension_semantics=("arbitrary",)),
        cost_estimate=cost,
    )(owners, flat_q, kv, kv, peak0, total0, mixed0, o_weight)


def shards(
    hidden_in,
    norm_gain,
    q_weight,
    q_bias,
    k_weight,
    k_bias,
    v_weight,
    v_bias,
    o_weight,
    prefix_kv,
    suffix_len,
    req_prefix,
    block_owner,
):
    length = hidden_in.shape[0]
    devices = lax.axis_size("req")
    owned = devices // NPREF
    block = prefix_kv.shape[0]
    prefix_len = block * owned
    kv_heads = k_weight.shape[1] // HD
    q_heads = q_weight.shape[1] // HD
    group = q_heads // kv_heads
    feat = hidden_in.shape[1]
    n_tp = lax.axis_size("tp")
    packed = jnp.concatenate(
        [hidden_in, norm_gain[None, :], jnp.zeros((ROWS - length - 1, feat), hidden_in.dtype)],
        axis=0,
    )
    spread = jnp.broadcast_to(packed[None], (n_tp,) + packed.shape)
    pieces_in = lax.all_to_all(spread, "tp", 0, 0, tiled=True)
    full = pieces_in.transpose(1, 0, 2).reshape(ROWS, n_tp * feat)
    tokens = full[:length].astype(jnp.float32)
    gain = full[length]
    meansq = jnp.mean(tokens * tokens, axis=-1, keepdims=True)
    normed = (tokens * lax.rsqrt(meansq + EPSILON) * gain.astype(jnp.float32)).astype(jnp.bfloat16)
    positions = prefix_len + jnp.arange(length, dtype=jnp.int32)
    queries = jnp.dot(normed, q_weight, preferred_element_type=jnp.float32) + q_bias.astype(
        jnp.float32
    )
    queries = rotate(queries.reshape(length, q_heads, HD), positions).astype(jnp.bfloat16)
    queries = queries.reshape(length, kv_heads, group, HD)
    keys = jnp.dot(normed, k_weight, preferred_element_type=jnp.float32) + k_bias.astype(
        jnp.float32
    )
    keys = rotate(keys.reshape(length, kv_heads, HD), positions).astype(jnp.bfloat16)
    values = jnp.dot(normed, v_weight, preferred_element_type=jnp.float32) + v_bias.astype(
        jnp.float32
    )
    values = values.astype(jnp.bfloat16).reshape(length, kv_heads, HD)
    slot_index = jnp.arange(length, dtype=jnp.int32)
    causal = slot_index[None, :] <= slot_index[:, None]
    peak, total, mixed = block_stats(queries, keys, values, causal)
    rows = length * q_heads
    peak0 = peak.reshape(length, q_heads).T.reshape(rows, 1)
    total0 = total.reshape(length, q_heads).T.reshape(rows, 1)
    mixed0 = mixed.reshape(length, q_heads, HD).transpose(1, 0, 2).reshape(rows, HD)
    which = req_prefix[0]
    rowwise = prefix_kv.reshape(block, 2 * kv_heads * HD)
    gathered = lax.all_gather(rowwise, "req", axis=0, tiled=True)
    stacked = gathered.reshape(devices, block, 2 * kv_heads * HD)
    owners = lax.dynamic_slice_in_dim(block_owner, which * owned, owned)
    pieces_out = prefix_attention(
        owners, queries.reshape(length, q_heads * HD), stacked, peak0, total0, mixed0,
        o_weight, n_tp,
    )
    summed = jnp.sum(lax.all_to_all(pieces_out, "tp", 0, 0, tiled=True).astype(jnp.float32), axis=0)
    valid = slot_index < suffix_len[0]
    return jnp.where(valid[:, None], summed, jnp.float32(0.0)).astype(jnp.bfloat16)


def solution(mesh):
    placed = (
        P("req", "tp"),
        P("tp"),
        P(None, "tp"),
        P("tp"),
        P(None, "tp"),
        P("tp"),
        P(None, "tp"),
        P("tp"),
        P("tp", None),
        P("req", None, "tp"),
        P("req"),
        P("req"),
        P(),
    )
    return jax.shard_map(
        shards, mesh=mesh, in_specs=placed, out_specs=P("req", "tp"), check_vma=False
    )
```

```python
import jax
import jax.numpy as jnp
from jax import lax
from jax.experimental import pallas as pl
from jax.experimental.pallas import tpu as pltpu
from jax.sharding import PartitionSpec as P

HD = 128
NPREF = 4


THETA = 1000000.0
EPSILON = 1e-06
ROWS = 144


def rotate(heads, positions):
    half = HD // 2
    freqs = THETA ** (-(jnp.arange(half, dtype=jnp.float32) * 2.0) / HD)
    angles = positions.astype(jnp.float32)[:, None] * freqs[None, :]
    cosine = jnp.cos(angles)[:, None, :]
    sine = jnp.sin(angles)[:, None, :]
    first = heads[..., :half]
    second = heads[..., half:]
    return jnp.concatenate(
        [first * cosine - second * sine, second * cosine + first * sine], axis=-1
    )


def block_stats(grouped, keys, values, allowed):
    scores = jnp.einsum(
        "sghd,kgd->sghk", grouped, keys, preferred_element_type=jnp.float32
    ) * HD ** (-0.5)
    if allowed is not None:
        scores = jnp.where(allowed[:, None, None, :], scores, -jnp.inf)
    peak = jnp.max(scores, axis=-1)
    weights = jnp.exp(scores - peak[..., None])
    total = jnp.sum(weights, axis=-1)
    mixed = jnp.einsum(
        "sghk,kgd->sghd", weights.astype(jnp.bfloat16), values, preferred_element_type=jnp.float32
    )
    return (peak, total, mixed)


def combine(first, second):
    peak = jnp.maximum(first[0], second[0])
    left = jnp.exp(first[0] - peak)
    right = jnp.exp(second[0] - peak)
    total = first[1] * left + second[1] * right
    mixed = first[2] * left[..., None] + second[2] * right[..., None]
    return (peak, total, mixed)


def prefix_kernel(
    own_ref, q_ref, k0_ref, v0_ref, k1_ref, v1_ref, m0_ref, l0_ref, a0_ref, w_hbm,
    o_ref, m_sc, l_sc, acc_sc, q_sc, w_sc, sem,
):
    step = pl.program_id(0)
    group = q_ref.shape[1] // HD
    fetch = pltpu.make_async_copy(w_hbm, w_sc, sem.at[0])

    @pl.when(step == 0)
    def _():
        fetch.start()
        m_sc[...] = m0_ref[...]
        l_sc[...] = l0_ref[...]
        acc_sc[...] = a0_ref[...]
        q = q_ref[...]
        q_sc[...] = jnp.concatenate([q[:, h * HD:(h + 1) * HD] for h in range(group)], axis=0)

    stacked = q_sc[...]
    dims = (((1,), (1,)), ((), ()))
    first = lax.dot_general(
        stacked, k0_ref[0], dims, preferred_element_type=jnp.float32
    ) * HD ** (-0.5)
    second = lax.dot_general(
        stacked, k1_ref[0], dims, preferred_element_type=jnp.float32
    ) * HD ** (-0.5)
    old = m_sc[...]
    new = jnp.maximum(
        old,
        jnp.maximum(jnp.max(first, axis=-1, keepdims=True), jnp.max(second, axis=-1, keepdims=True)),
    )
    alpha = jnp.exp(old - new)
    w0 = jnp.exp(first - new)
    w1 = jnp.exp(second - new)
    l_sc[...] = alpha * l_sc[...] + (
        jnp.sum(w0, axis=-1, keepdims=True) + jnp.sum(w1, axis=-1, keepdims=True)
    )
    acc_sc[...] = alpha * acc_sc[...] + (
        jnp.dot(w0.astype(jnp.bfloat16), v0_ref[0], preferred_element_type=jnp.float32)
        + jnp.dot(w1.astype(jnp.bfloat16), v1_ref[0], preferred_element_type=jnp.float32)
    )
    m_sc[...] = new

    @pl.when(step == pl.num_programs(0) - 1)
    def _():
        context = (acc_sc[...] / l_sc[...]).astype(jnp.bfloat16)
        rows = q_ref.shape[0]
        flat = jnp.concatenate([context[h * rows:(h + 1) * rows] for h in range(group)], axis=1)
        fetch.wait()
        partial = jnp.dot(flat, w_sc[...], preferred_element_type=jnp.float32).astype(o_ref.dtype)
        pieces = o_ref.shape[0]
        span = o_ref.shape[2]
        for t in range(pieces):
            o_ref[t] = partial[:, t * span:(t + 1) * span]


def prefix_attention(owners, flat_q, kv, peak0, total0, mixed0, o_weight, pieces):
    length, width = flat_q.shape
    out_width = o_weight.shape[1]
    steps = owners.shape[0]
    block = kv.shape[1]
    rows = peak0.shape[0]
    cost = pl.CostEstimate(
        flops=4 * rows * block * HD * steps,
        transcendentals=rows * block * steps,
        bytes_accessed=2 * steps * block * HD * 2 + length * width * 4 + rows * HD * 4
        + width * out_width * 2 + length * out_width * 2,
    )
    return pl.pallas_call(
        prefix_kernel,
        out_shape=jax.ShapeDtypeStruct((pieces, length, out_width // pieces), jnp.bfloat16),
        grid_spec=pltpu.PrefetchScalarGridSpec(
            num_scalar_prefetch=1,
            grid=(steps // 2,),
            in_specs=[
                pl.BlockSpec((length, width), lambda j, own: (0, 0)),
                pl.BlockSpec((1, block, HD), lambda j, own: (own[2 * j], 0, 0)),
                pl.BlockSpec((1, block, HD), lambda j, own: (own[2 * j], 0, 1)),
                pl.BlockSpec((1, block, HD), lambda j, own: (own[2 * j + 1], 0, 0)),
                pl.BlockSpec((1, block, HD), lambda j, own: (own[2 * j + 1], 0, 1)),
                pl.BlockSpec((rows, 1), lambda j, own: (0, 0)),
                pl.BlockSpec((rows, 1), lambda j, own: (0, 0)),
                pl.BlockSpec((rows, HD), lambda j, own: (0, 0)),
                pl.BlockSpec(memory_space=pl.ANY),
            ],
            out_specs=pl.BlockSpec((pieces, length, out_width // pieces), lambda j, own: (0, 0, 0)),
            scratch_shapes=[
                pltpu.VMEM((rows, 1), jnp.float32),
                pltpu.VMEM((rows, 1), jnp.float32),
                pltpu.VMEM((rows, HD), jnp.float32),
                pltpu.VMEM((rows, HD), jnp.bfloat16),
                pltpu.VMEM((width, out_width), jnp.bfloat16),
                pltpu.SemaphoreType.DMA((1,)),
            ],
        ),
        compiler_params=pltpu.CompilerParams(dimension_semantics=("arbitrary",)),
        cost_estimate=cost,
    )(owners, flat_q, kv, kv, kv, kv, peak0, total0, mixed0, o_weight)


def shards(
    hidden_in,
    norm_gain,
    q_weight,
    q_bias,
    k_weight,
    k_bias,
    v_weight,
    v_bias,
    o_weight,
    prefix_kv,
    suffix_len,
    req_prefix,
    block_owner,
):
    length = hidden_in.shape[0]
    devices = lax.axis_size("req")
    owned = devices // NPREF
    block = prefix_kv.shape[0]
    prefix_len = block * owned
    kv_heads = k_weight.shape[1] // HD
    q_heads = q_weight.shape[1] // HD
    group = q_heads // kv_heads
    feat = hidden_in.shape[1]
    n_tp = lax.axis_size("tp")
    packed = jnp.concatenate(
        [hidden_in, norm_gain[None, :], jnp.zeros((ROWS - length - 1, feat), hidden_in.dtype)],
        axis=0,
    )
    spread = jnp.broadcast_to(packed[None], (n_tp,) + packed.shape)
    pieces_in = lax.all_to_all(spread, "tp", 0, 0, tiled=True)
    full = pieces_in.transpose(1, 0, 2).reshape(ROWS, n_tp * feat)
    tokens = full[:length].astype(jnp.float32)
    gain = full[length]
    meansq = jnp.mean(tokens * tokens, axis=-1, keepdims=True)
    normed = (tokens * lax.rsqrt(meansq + EPSILON) * gain.astype(jnp.float32)).astype(jnp.bfloat16)
    positions = prefix_len + jnp.arange(length, dtype=jnp.int32)
    queries = jnp.dot(normed, q_weight, preferred_element_type=jnp.float32) + q_bias.astype(
        jnp.float32
    )
    queries = rotate(queries.reshape(length, q_heads, HD), positions).astype(jnp.bfloat16)
    queries = queries.reshape(length, kv_heads, group, HD)
    keys = jnp.dot(normed, k_weight, preferred_element_type=jnp.float32) + k_bias.astype(
        jnp.float32
    )
    keys = rotate(keys.reshape(length, kv_heads, HD), positions).astype(jnp.bfloat16)
    values = jnp.dot(normed, v_weight, preferred_element_type=jnp.float32) + v_bias.astype(
        jnp.float32
    )
    values = values.astype(jnp.bfloat16).reshape(length, kv_heads, HD)
    slot_index = jnp.arange(length, dtype=jnp.int32)
    causal = slot_index[None, :] <= slot_index[:, None]
    peak, total, mixed = block_stats(queries, keys, values, causal)
    rows = length * q_heads
    peak0 = peak.reshape(length, q_heads).T.reshape(rows, 1)
    total0 = total.reshape(length, q_heads).T.reshape(rows, 1)
    mixed0 = mixed.reshape(length, q_heads, HD).transpose(1, 0, 2).reshape(rows, HD)
    which = req_prefix[0]
    rowwise = prefix_kv.reshape(block, 2 * kv_heads * HD)
    gathered = lax.all_gather(rowwise, "req", axis=0, tiled=True)
    stacked = gathered.reshape(devices, block, 2 * kv_heads * HD)
    owners = lax.dynamic_slice_in_dim(block_owner, which * owned, owned)
    pieces_out = prefix_attention(
        owners, queries.reshape(length, q_heads * HD), stacked, peak0, total0, mixed0,
        o_weight, n_tp,
    )
    summed = jnp.sum(lax.all_to_all(pieces_out, "tp", 0, 0, tiled=True).astype(jnp.float32), axis=0)
    valid = slot_index < suffix_len[0]
    return jnp.where(valid[:, None], summed, jnp.float32(0.0)).astype(jnp.bfloat16)


def solution(mesh):
    placed = (
        P("req", "tp"),
        P("tp"),
        P(None, "tp"),
        P("tp"),
        P(None, "tp"),
        P("tp"),
        P(None, "tp"),
        P("tp"),
        P("tp", None),
        P("req", None, "tp"),
        P("req"),
        P("req"),
        P(),
    )
    return jax.shard_map(
        shards, mesh=mesh, in_specs=placed, out_specs=P("req", "tp"), check_vma=False
    )
```

```python
import jax
import jax.numpy as jnp
from jax import lax
from jax.experimental import pallas as pl
from jax.experimental.pallas import tpu as pltpu
from jax.sharding import PartitionSpec as P

HD = 128
NPREF = 4


THETA = 1000000.0
EPSILON = 1e-06
ROWS = 144


def rotate(heads, positions):
    half = HD // 2
    freqs = THETA ** (-(jnp.arange(half, dtype=jnp.float32) * 2.0) / HD)
    angles = positions.astype(jnp.float32)[:, None] * freqs[None, :]
    cosine = jnp.cos(angles)[:, None, :]
    sine = jnp.sin(angles)[:, None, :]
    first = heads[..., :half]
    second = heads[..., half:]
    return jnp.concatenate(
        [first * cosine - second * sine, second * cosine + first * sine], axis=-1
    )


def block_stats(grouped, keys, values, allowed):
    scores = jnp.einsum(
        "sghd,kgd->sghk", grouped, keys, preferred_element_type=jnp.float32
    ) * HD ** (-0.5)
    if allowed is not None:
        scores = jnp.where(allowed[:, None, None, :], scores, -jnp.inf)
    peak = jnp.max(scores, axis=-1)
    weights = jnp.exp(scores - peak[..., None])
    total = jnp.sum(weights, axis=-1)
    mixed = jnp.einsum(
        "sghk,kgd->sghd", weights.astype(jnp.bfloat16), values, preferred_element_type=jnp.float32
    )
    return (peak, total, mixed)


def combine(first, second):
    peak = jnp.maximum(first[0], second[0])
    left = jnp.exp(first[0] - peak)
    right = jnp.exp(second[0] - peak)
    total = first[1] * left + second[1] * right
    mixed = first[2] * left[..., None] + second[2] * right[..., None]
    return (peak, total, mixed)


def prefix_kernel(
    own_ref, q_ref, k0_ref, k1_ref, m0_ref, l0_ref, a0_ref, w_hbm,
    o_ref, m_sc, l_sc, acc_sc, q_sc, w_sc, sem,
):
    step = pl.program_id(0)
    group = q_ref.shape[1] // HD
    fetch = pltpu.make_async_copy(w_hbm, w_sc, sem.at[0])

    @pl.when(step == 0)
    def _():
        fetch.start()
        m_sc[...] = m0_ref[...]
        l_sc[...] = l0_ref[...]
        acc_sc[...] = a0_ref[...]
        q = q_ref[...]
        q_sc[...] = jnp.concatenate([q[:, h * HD:(h + 1) * HD] for h in range(group)], axis=0)

    stacked = q_sc[...]
    dims = (((1,), (1,)), ((), ()))
    kv0 = k0_ref[...]
    kv1 = k1_ref[...]
    first = lax.dot_general(
        stacked, kv0[:, 0, :], dims, preferred_element_type=jnp.float32
    ) * HD ** (-0.5)
    second = lax.dot_general(
        stacked, kv1[:, 0, :], dims, preferred_element_type=jnp.float32
    ) * HD ** (-0.5)
    old = m_sc[...]
    new = jnp.maximum(
        old,
        jnp.maximum(jnp.max(first, axis=-1, keepdims=True), jnp.max(second, axis=-1, keepdims=True)),
    )
    alpha = jnp.exp(old - new)
    w0 = jnp.exp(first - new)
    w1 = jnp.exp(second - new)
    l_sc[...] = alpha * l_sc[...] + (
        jnp.sum(w0, axis=-1, keepdims=True) + jnp.sum(w1, axis=-1, keepdims=True)
    )
    acc_sc[...] = alpha * acc_sc[...] + (
        jnp.dot(w0.astype(jnp.bfloat16), kv0[:, 1, :], preferred_element_type=jnp.float32)
        + jnp.dot(w1.astype(jnp.bfloat16), kv1[:, 1, :], preferred_element_type=jnp.float32)
    )
    m_sc[...] = new

    @pl.when(step == pl.num_programs(0) - 1)
    def _():
        context = (acc_sc[...] / l_sc[...]).astype(jnp.bfloat16)
        rows = q_ref.shape[0]
        flat = jnp.concatenate([context[h * rows:(h + 1) * rows] for h in range(group)], axis=1)
        fetch.wait()
        partial = jnp.dot(flat, w_sc[...], preferred_element_type=jnp.float32).astype(o_ref.dtype)
        pieces = o_ref.shape[0]
        span = o_ref.shape[2]
        for t in range(pieces):
            o_ref[t] = partial[:, t * span:(t + 1) * span]


def prefix_attention(owners, flat_q, kv, peak0, total0, mixed0, o_weight, pieces):
    length, width = flat_q.shape
    out_width = o_weight.shape[1]
    steps = owners.shape[0]
    block = kv.shape[0] // steps // NPREF
    rows = peak0.shape[0]
    cost = pl.CostEstimate(
        flops=4 * rows * block * HD * steps,
        transcendentals=rows * block * steps,
        bytes_accessed=2 * steps * block * HD * 2 + length * width * 4 + rows * HD * 4
        + width * out_width * 2 + length * out_width * 2,
    )
    return pl.pallas_call(
        prefix_kernel,
        out_shape=jax.ShapeDtypeStruct((pieces, length, out_width // pieces), jnp.bfloat16),
        grid_spec=pltpu.PrefetchScalarGridSpec(
            num_scalar_prefetch=1,
            grid=(steps // 2,),
            in_specs=[
                pl.BlockSpec((length, width), lambda j, own: (0, 0)),
                pl.BlockSpec((block, 2, HD), lambda j, own: (own[2 * j], 0, 0)),
                pl.BlockSpec((block, 2, HD), lambda j, own: (own[2 * j + 1], 0, 0)),
                pl.BlockSpec((rows, 1), lambda j, own: (0, 0)),
                pl.BlockSpec((rows, 1), lambda j, own: (0, 0)),
                pl.BlockSpec((rows, HD), lambda j, own: (0, 0)),
                pl.BlockSpec(memory_space=pl.ANY),
            ],
            out_specs=pl.BlockSpec((pieces, length, out_width // pieces), lambda j, own: (0, 0, 0)),
            scratch_shapes=[
                pltpu.VMEM((rows, 1), jnp.float32),
                pltpu.VMEM((rows, 1), jnp.float32),
                pltpu.VMEM((rows, HD), jnp.float32),
                pltpu.VMEM((rows, HD), jnp.bfloat16),
                pltpu.VMEM((width, out_width), jnp.bfloat16),
                pltpu.SemaphoreType.DMA((1,)),
            ],
        ),
        compiler_params=pltpu.CompilerParams(dimension_semantics=("arbitrary",)),
        cost_estimate=cost,
    )(owners, flat_q, kv, kv, peak0, total0, mixed0, o_weight)


def shards(
    hidden_in,
    norm_gain,
    q_weight,
    q_bias,
    k_weight,
    k_bias,
    v_weight,
    v_bias,
    o_weight,
    prefix_kv,
    suffix_len,
    req_prefix,
    block_owner,
):
    length = hidden_in.shape[0]
    devices = lax.axis_size("req")
    owned = devices // NPREF
    block = prefix_kv.shape[0]
    prefix_len = block * owned
    kv_heads = k_weight.shape[1] // HD
    q_heads = q_weight.shape[1] // HD
    group = q_heads // kv_heads
    feat = hidden_in.shape[1]
    n_tp = lax.axis_size("tp")
    packed = jnp.concatenate(
        [hidden_in, norm_gain[None, :], jnp.zeros((ROWS - length - 1, feat), hidden_in.dtype)],
        axis=0,
    )
    spread = jnp.broadcast_to(packed[None], (n_tp,) + packed.shape)
    pieces_in = lax.all_to_all(spread, "tp", 0, 0, tiled=True)
    full = pieces_in.transpose(1, 0, 2).reshape(ROWS, n_tp * feat)
    tokens = full[:length].astype(jnp.float32)
    gain = full[length]
    meansq = jnp.mean(tokens * tokens, axis=-1, keepdims=True)
    normed = (tokens * lax.rsqrt(meansq + EPSILON) * gain.astype(jnp.float32)).astype(jnp.bfloat16)
    positions = prefix_len + jnp.arange(length, dtype=jnp.int32)
    queries = jnp.dot(normed, q_weight, preferred_element_type=jnp.float32) + q_bias.astype(
        jnp.float32
    )
    queries = rotate(queries.reshape(length, q_heads, HD), positions).astype(jnp.bfloat16)
    queries = queries.reshape(length, kv_heads, group, HD)
    keys = jnp.dot(normed, k_weight, preferred_element_type=jnp.float32) + k_bias.astype(
        jnp.float32
    )
    keys = rotate(keys.reshape(length, kv_heads, HD), positions).astype(jnp.bfloat16)
    values = jnp.dot(normed, v_weight, preferred_element_type=jnp.float32) + v_bias.astype(
        jnp.float32
    )
    values = values.astype(jnp.bfloat16).reshape(length, kv_heads, HD)
    slot_index = jnp.arange(length, dtype=jnp.int32)
    causal = slot_index[None, :] <= slot_index[:, None]
    peak, total, mixed = block_stats(queries, keys, values, causal)
    rows = length * q_heads
    peak0 = peak.reshape(length, q_heads).T.reshape(rows, 1)
    total0 = total.reshape(length, q_heads).T.reshape(rows, 1)
    mixed0 = mixed.reshape(length, q_heads, HD).transpose(1, 0, 2).reshape(rows, HD)
    which = req_prefix[0]
    stacked = lax.all_gather(prefix_kv, "req", axis=0, tiled=True)
    owners = lax.dynamic_slice_in_dim(block_owner, which * owned, owned)
    pieces_out = prefix_attention(
        owners, queries.reshape(length, q_heads * HD), stacked, peak0, total0, mixed0,
        o_weight, n_tp,
    )
    summed = jnp.sum(lax.all_to_all(pieces_out, "tp", 0, 0, tiled=True).astype(jnp.float32), axis=0)
    valid = slot_index < suffix_len[0]
    return jnp.where(valid[:, None], summed, jnp.float32(0.0)).astype(jnp.bfloat16)


def solution(mesh):
    placed = (
        P("req", "tp"),
        P("tp"),
        P(None, "tp"),
        P("tp"),
        P(None, "tp"),
        P("tp"),
        P(None, "tp"),
        P("tp"),
        P("tp", None),
        P("req", None, "tp"),
        P("req"),
        P("req"),
        P(),
    )
    return jax.shard_map(
        shards, mesh=mesh, in_specs=placed, out_specs=P("req", "tp"), check_vma=False
    )
```

```python
import jax
import jax.numpy as jnp
from jax import lax
from jax.experimental import pallas as pl
from jax.experimental.pallas import tpu as pltpu
from jax.sharding import PartitionSpec as P

HD = 128
NPREF = 4


THETA = 1000000.0
EPSILON = 1e-06
ROWS = 144
PER_STEP = 4


def rotate(heads, positions):
    half = HD // 2
    freqs = THETA ** (-(jnp.arange(half, dtype=jnp.float32) * 2.0) / HD)
    angles = positions.astype(jnp.float32)[:, None] * freqs[None, :]
    cosine = jnp.cos(angles)[:, None, :]
    sine = jnp.sin(angles)[:, None, :]
    first = heads[..., :half]
    second = heads[..., half:]
    return jnp.concatenate(
        [first * cosine - second * sine, second * cosine + first * sine], axis=-1
    )


def block_stats(grouped, keys, values, allowed):
    scores = jnp.einsum(
        "sghd,kgd->sghk", grouped, keys, preferred_element_type=jnp.float32
    ) * HD ** (-0.5)
    if allowed is not None:
        scores = jnp.where(allowed[:, None, None, :], scores, -jnp.inf)
    peak = jnp.max(scores, axis=-1)
    weights = jnp.exp(scores - peak[..., None])
    total = jnp.sum(weights, axis=-1)
    mixed = jnp.einsum(
        "sghk,kgd->sghd", weights.astype(jnp.bfloat16), values, preferred_element_type=jnp.float32
    )
    return (peak, total, mixed)


def combine(first, second):
    peak = jnp.maximum(first[0], second[0])
    left = jnp.exp(first[0] - peak)
    right = jnp.exp(second[0] - peak)
    total = first[1] * left + second[1] * right
    mixed = first[2] * left[..., None] + second[2] * right[..., None]
    return (peak, total, mixed)


def prefix_kernel(own_ref, q_ref, *refs):
    kv_refs = refs[:2 * PER_STEP]
    m0_ref, l0_ref, a0_ref, w_hbm, o_ref, m_sc, l_sc, acc_sc, q_sc, w_sc, sem = refs[2 * PER_STEP:]
    step = pl.program_id(0)
    group = q_ref.shape[1] // HD
    fetch = pltpu.make_async_copy(w_hbm, w_sc, sem.at[0])

    @pl.when(step == 0)
    def _():
        fetch.start()
        m_sc[...] = m0_ref[...]
        l_sc[...] = l0_ref[...]
        acc_sc[...] = a0_ref[...]
        q = q_ref[...]
        q_sc[...] = jnp.concatenate([q[:, h * HD:(h + 1) * HD] for h in range(group)], axis=0)

    stacked = q_sc[...]
    dims = (((1,), (1,)), ((), ()))
    refs = kv_refs
    parts = [
        lax.dot_general(stacked, refs[2 * i][0], dims, preferred_element_type=jnp.float32)
        * HD ** (-0.5)
        for i in range(len(refs) // 2)
    ]
    old = m_sc[...]
    top = old
    for part in parts:
        top = jnp.maximum(top, jnp.max(part, axis=-1, keepdims=True))
    alpha = jnp.exp(old - top)
    weights = [jnp.exp(part - top) for part in parts]
    summed = weights[0].sum(axis=-1, keepdims=True)
    mixed = jnp.dot(weights[0].astype(jnp.bfloat16), refs[1][0], preferred_element_type=jnp.float32)
    for i in range(1, len(weights)):
        summed = summed + weights[i].sum(axis=-1, keepdims=True)
        mixed = mixed + jnp.dot(
            weights[i].astype(jnp.bfloat16), refs[2 * i + 1][0], preferred_element_type=jnp.float32
        )
    l_sc[...] = alpha * l_sc[...] + summed
    acc_sc[...] = alpha * acc_sc[...] + mixed
    m_sc[...] = top

    @pl.when(step == pl.num_programs(0) - 1)
    def _():
        context = (acc_sc[...] / l_sc[...]).astype(jnp.bfloat16)
        rows = q_ref.shape[0]
        flat = jnp.concatenate([context[h * rows:(h + 1) * rows] for h in range(group)], axis=1)
        fetch.wait()
        partial = jnp.dot(flat, w_sc[...], preferred_element_type=jnp.float32).astype(o_ref.dtype)
        pieces = o_ref.shape[0]
        span = o_ref.shape[2]
        for t in range(pieces):
            o_ref[t] = partial[:, t * span:(t + 1) * span]


def prefix_attention(owners, flat_q, kv, peak0, total0, mixed0, o_weight, pieces):
    length, width = flat_q.shape
    out_width = o_weight.shape[1]
    steps = owners.shape[0]
    block = kv.shape[1]
    rows = peak0.shape[0]
    cost = pl.CostEstimate(
        flops=4 * rows * block * HD * steps,
        transcendentals=rows * block * steps,
        bytes_accessed=2 * steps * block * HD * 2 + length * width * 4 + rows * HD * 4
        + width * out_width * 2 + length * out_width * 2,
    )
    return pl.pallas_call(
        prefix_kernel,
        out_shape=jax.ShapeDtypeStruct((pieces, length, out_width // pieces), jnp.bfloat16),
        grid_spec=pltpu.PrefetchScalarGridSpec(
            num_scalar_prefetch=1,
            grid=(steps // PER_STEP,),
            in_specs=[
                pl.BlockSpec((length, width), lambda j, own: (0, 0)),
                *[
                    pl.BlockSpec((1, block, HD), lambda j, own, i=i, c=c: (own[PER_STEP * j + i], 0, c))
                    for i in range(PER_STEP)
                    for c in range(2)
                ],
                pl.BlockSpec((rows, 1), lambda j, own: (0, 0)),
                pl.BlockSpec((rows, 1), lambda j, own: (0, 0)),
                pl.BlockSpec((rows, HD), lambda j, own: (0, 0)),
                pl.BlockSpec(memory_space=pl.ANY),
            ],
            out_specs=pl.BlockSpec((pieces, length, out_width // pieces), lambda j, own: (0, 0, 0)),
            scratch_shapes=[
                pltpu.VMEM((rows, 1), jnp.float32),
                pltpu.VMEM((rows, 1), jnp.float32),
                pltpu.VMEM((rows, HD), jnp.float32),
                pltpu.VMEM((rows, HD), jnp.bfloat16),
                pltpu.VMEM((width, out_width), jnp.bfloat16),
                pltpu.SemaphoreType.DMA((1,)),
            ],
        ),
        compiler_params=pltpu.CompilerParams(dimension_semantics=("arbitrary",)),
        cost_estimate=cost,
    )(owners, flat_q, *([kv] * (2 * PER_STEP)), peak0, total0, mixed0, o_weight)


def shards(
    hidden_in,
    norm_gain,
    q_weight,
    q_bias,
    k_weight,
    k_bias,
    v_weight,
    v_bias,
    o_weight,
    prefix_kv,
    suffix_len,
    req_prefix,
    block_owner,
):
    length = hidden_in.shape[0]
    devices = lax.axis_size("req")
    owned = devices // NPREF
    block = prefix_kv.shape[0]
    prefix_len = block * owned
    kv_heads = k_weight.shape[1] // HD
    q_heads = q_weight.shape[1] // HD
    group = q_heads // kv_heads
    feat = hidden_in.shape[1]
    n_tp = lax.axis_size("tp")
    packed = jnp.concatenate(
        [hidden_in, norm_gain[None, :], jnp.zeros((ROWS - length - 1, feat), hidden_in.dtype)],
        axis=0,
    )
    spread = jnp.broadcast_to(packed[None], (n_tp,) + packed.shape)
    pieces_in = lax.all_to_all(spread, "tp", 0, 0, tiled=True)
    full = pieces_in.transpose(1, 0, 2).reshape(ROWS, n_tp * feat)
    tokens = full[:length].astype(jnp.float32)
    gain = full[length]
    meansq = jnp.mean(tokens * tokens, axis=-1, keepdims=True)
    normed = (tokens * lax.rsqrt(meansq + EPSILON) * gain.astype(jnp.float32)).astype(jnp.bfloat16)
    positions = prefix_len + jnp.arange(length, dtype=jnp.int32)
    queries = jnp.dot(normed, q_weight, preferred_element_type=jnp.float32) + q_bias.astype(
        jnp.float32
    )
    queries = rotate(queries.reshape(length, q_heads, HD), positions).astype(jnp.bfloat16)
    queries = queries.reshape(length, kv_heads, group, HD)
    keys = jnp.dot(normed, k_weight, preferred_element_type=jnp.float32) + k_bias.astype(
        jnp.float32
    )
    keys = rotate(keys.reshape(length, kv_heads, HD), positions).astype(jnp.bfloat16)
    values = jnp.dot(normed, v_weight, preferred_element_type=jnp.float32) + v_bias.astype(
        jnp.float32
    )
    values = values.astype(jnp.bfloat16).reshape(length, kv_heads, HD)
    slot_index = jnp.arange(length, dtype=jnp.int32)
    causal = slot_index[None, :] <= slot_index[:, None]
    peak, total, mixed = block_stats(queries, keys, values, causal)
    rows = length * q_heads
    peak0 = peak.reshape(length, q_heads).T.reshape(rows, 1)
    total0 = total.reshape(length, q_heads).T.reshape(rows, 1)
    mixed0 = mixed.reshape(length, q_heads, HD).transpose(1, 0, 2).reshape(rows, HD)
    which = req_prefix[0]
    rowwise = prefix_kv.reshape(block, 2 * kv_heads * HD)
    gathered = lax.all_gather(rowwise, "req", axis=0, tiled=True)
    stacked = gathered.reshape(devices, block, 2 * kv_heads * HD)
    owners = lax.dynamic_slice_in_dim(block_owner, which * owned, owned)
    pieces_out = prefix_attention(
        owners, queries.reshape(length, q_heads * HD), stacked, peak0, total0, mixed0,
        o_weight, n_tp,
    )
    summed = jnp.sum(lax.all_to_all(pieces_out, "tp", 0, 0, tiled=True).astype(jnp.float32), axis=0)
    valid = slot_index < suffix_len[0]
    return jnp.where(valid[:, None], summed, jnp.float32(0.0)).astype(jnp.bfloat16)


def solution(mesh):
    placed = (
        P("req", "tp"),
        P("tp"),
        P(None, "tp"),
        P("tp"),
        P(None, "tp"),
        P("tp"),
        P(None, "tp"),
        P("tp"),
        P("tp", None),
        P("req", None, "tp"),
        P("req"),
        P("req"),
        P(),
    )
    return jax.shard_map(
        shards, mesh=mesh, in_specs=placed, out_specs=P("req", "tp"), check_vma=False
    )
```

```python
import jax
import jax.numpy as jnp
from jax import lax
from jax.experimental import pallas as pl
from jax.experimental.pallas import tpu as pltpu
from jax.sharding import PartitionSpec as P

HD = 128
NPREF = 4


THETA = 1000000.0
EPSILON = 1e-06
ROWS = 144
PER_STEP = 4


def rotate(heads, positions):
    half = HD // 2
    freqs = THETA ** (-(jnp.arange(half, dtype=jnp.float32) * 2.0) / HD)
    angles = positions.astype(jnp.float32)[:, None] * freqs[None, :]
    cosine = jnp.cos(angles)[:, None, :]
    sine = jnp.sin(angles)[:, None, :]
    first = heads[..., :half]
    second = heads[..., half:]
    return jnp.concatenate(
        [first * cosine - second * sine, second * cosine + first * sine], axis=-1
    )


def block_stats(grouped, keys, values, allowed):
    scores = jnp.einsum(
        "sghd,kgd->sghk", grouped, keys, preferred_element_type=jnp.float32
    ) * HD ** (-0.5)
    if allowed is not None:
        scores = jnp.where(allowed[:, None, None, :], scores, -jnp.inf)
    peak = jnp.max(scores, axis=-1)
    weights = jnp.exp(scores - peak[..., None])
    total = jnp.sum(weights, axis=-1)
    mixed = jnp.einsum(
        "sghk,kgd->sghd", weights.astype(jnp.bfloat16), values, preferred_element_type=jnp.float32
    )
    return (peak, total, mixed)


def combine(first, second):
    peak = jnp.maximum(first[0], second[0])
    left = jnp.exp(first[0] - peak)
    right = jnp.exp(second[0] - peak)
    total = first[1] * left + second[1] * right
    mixed = first[2] * left[..., None] + second[2] * right[..., None]
    return (peak, total, mixed)


def prefix_kernel(own_ref, q_ref, *refs):
    kv_refs = refs[:2 * PER_STEP]
    m0_ref, l0_ref, a0_ref, w_hbm, o_ref, m_sc, l_sc, acc_sc, q_sc, w_sc, sem = refs[2 * PER_STEP:]
    step = pl.program_id(0)
    group = q_ref.shape[1] // HD
    fetch = pltpu.make_async_copy(w_hbm, w_sc, sem.at[0])

    @pl.when(step == 0)
    def _():
        fetch.start()
        m_sc[...] = m0_ref[...]
        l_sc[...] = l0_ref[...]
        acc_sc[...] = a0_ref[...]
        q = q_ref[...]
        q_sc[...] = jnp.concatenate([q[:, h * HD:(h + 1) * HD] for h in range(group)], axis=0)

    stacked = q_sc[...]
    dims = (((1,), (1,)), ((), ()))
    refs = kv_refs
    parts = [
        lax.dot_general(stacked, refs[2 * i][0], dims, preferred_element_type=jnp.float32)
        * HD ** (-0.5)
        for i in range(len(refs) // 2)
    ]
    old = m_sc[...]
    top = old
    for part in parts:
        top = jnp.maximum(top, jnp.max(part, axis=-1, keepdims=True))
    alpha = jnp.exp(old - top)
    weights = [jnp.exp(part - top) for part in parts]
    summed = weights[0].sum(axis=-1, keepdims=True)
    mixed = jnp.dot(weights[0].astype(jnp.bfloat16), refs[1][0], preferred_element_type=jnp.float32)
    for i in range(1, len(weights)):
        summed = summed + weights[i].sum(axis=-1, keepdims=True)
        mixed = mixed + jnp.dot(
            weights[i].astype(jnp.bfloat16), refs[2 * i + 1][0], preferred_element_type=jnp.float32
        )
    l_sc[...] = alpha * l_sc[...] + summed
    acc_sc[...] = alpha * acc_sc[...] + mixed
    m_sc[...] = top

    @pl.when(step == pl.num_programs(0) - 1)
    def _():
        context = (acc_sc[...] / l_sc[...]).astype(jnp.bfloat16)
        rows = q_ref.shape[0]
        flat = jnp.concatenate([context[h * rows:(h + 1) * rows] for h in range(group)], axis=1)
        fetch.wait()
        partial = jnp.dot(flat, w_sc[...], preferred_element_type=jnp.float32).astype(o_ref.dtype)
        pieces = o_ref.shape[0]
        span = o_ref.shape[2]
        for t in range(pieces):
            o_ref[t] = partial[:, t * span:(t + 1) * span]


def prefix_attention(owners, flat_q, kv, peak0, total0, mixed0, o_weight, pieces):
    length, width = flat_q.shape
    out_width = o_weight.shape[1]
    steps = owners.shape[0]
    block = kv.shape[1]
    rows = peak0.shape[0]
    cost = pl.CostEstimate(
        flops=4 * rows * block * HD * steps,
        transcendentals=rows * block * steps,
        bytes_accessed=2 * steps * block * HD * 2 + length * width * 4 + rows * HD * 4
        + width * out_width * 2 + length * out_width * 2,
    )
    return pl.pallas_call(
        prefix_kernel,
        out_shape=jax.ShapeDtypeStruct((pieces, length, out_width // pieces), jnp.bfloat16),
        grid_spec=pltpu.PrefetchScalarGridSpec(
            num_scalar_prefetch=1,
            grid=(steps // PER_STEP,),
            in_specs=[
                pl.BlockSpec((length, width), lambda j, own: (0, 0)),
                *[
                    pl.BlockSpec((1, block, HD), lambda j, own, i=i, c=c: (own[PER_STEP * j + i], 0, c))
                    for i in range(PER_STEP)
                    for c in range(2)
                ],
                pl.BlockSpec((rows, 1), lambda j, own: (0, 0)),
                pl.BlockSpec((rows, 1), lambda j, own: (0, 0)),
                pl.BlockSpec((rows, HD), lambda j, own: (0, 0)),
                pl.BlockSpec(memory_space=pl.ANY),
            ],
            out_specs=pl.BlockSpec((pieces, length, out_width // pieces), lambda j, own: (0, 0, 0)),
            scratch_shapes=[
                pltpu.VMEM((rows, 1), jnp.float32),
                pltpu.VMEM((rows, 1), jnp.float32),
                pltpu.VMEM((rows, HD), jnp.float32),
                pltpu.VMEM((rows, HD), jnp.bfloat16),
                pltpu.VMEM((width, out_width), jnp.bfloat16),
                pltpu.SemaphoreType.DMA((1,)),
            ],
        ),
        compiler_params=pltpu.CompilerParams(dimension_semantics=("arbitrary",)),
        cost_estimate=cost,
    )(owners, flat_q, *([kv] * (2 * PER_STEP)), peak0, total0, mixed0, o_weight)


def shards(
    hidden_in,
    norm_gain,
    q_weight,
    q_bias,
    k_weight,
    k_bias,
    v_weight,
    v_bias,
    o_weight,
    prefix_kv,
    suffix_len,
    req_prefix,
    block_owner,
):
    length = hidden_in.shape[0]
    devices = lax.axis_size("req")
    owned = devices // NPREF
    block = prefix_kv.shape[0]
    prefix_len = block * owned
    kv_heads = k_weight.shape[1] // HD
    q_heads = q_weight.shape[1] // HD
    group = q_heads // kv_heads
    feat = hidden_in.shape[1]
    n_tp = lax.axis_size("tp")
    packed = jnp.concatenate(
        [hidden_in, norm_gain[None, :], jnp.zeros((ROWS - length - 1, feat), hidden_in.dtype)],
        axis=0,
    )
    me_tp = lax.axis_index("tp")
    by_shift = jnp.stack(
        [packed]
        + [
            lax.ppermute(packed, "tp", [(i, (i + s) % n_tp) for i in range(n_tp)])
            for s in range(1, n_tp)
        ]
    )
    pieces_in = jnp.take(by_shift, (me_tp - jnp.arange(n_tp, dtype=jnp.int32)) % n_tp, axis=0)
    full = pieces_in.transpose(1, 0, 2).reshape(ROWS, n_tp * feat)
    tokens = full[:length].astype(jnp.float32)
    gain = full[length]
    meansq = jnp.mean(tokens * tokens, axis=-1, keepdims=True)
    normed = (tokens * lax.rsqrt(meansq + EPSILON) * gain.astype(jnp.float32)).astype(jnp.bfloat16)
    positions = prefix_len + jnp.arange(length, dtype=jnp.int32)
    queries = jnp.dot(normed, q_weight, preferred_element_type=jnp.float32) + q_bias.astype(
        jnp.float32
    )
    queries = rotate(queries.reshape(length, q_heads, HD), positions).astype(jnp.bfloat16)
    queries = queries.reshape(length, kv_heads, group, HD)
    keys = jnp.dot(normed, k_weight, preferred_element_type=jnp.float32) + k_bias.astype(
        jnp.float32
    )
    keys = rotate(keys.reshape(length, kv_heads, HD), positions).astype(jnp.bfloat16)
    values = jnp.dot(normed, v_weight, preferred_element_type=jnp.float32) + v_bias.astype(
        jnp.float32
    )
    values = values.astype(jnp.bfloat16).reshape(length, kv_heads, HD)
    slot_index = jnp.arange(length, dtype=jnp.int32)
    causal = slot_index[None, :] <= slot_index[:, None]
    peak, total, mixed = block_stats(queries, keys, values, causal)
    rows = length * q_heads
    peak0 = peak.reshape(length, q_heads).T.reshape(rows, 1)
    total0 = total.reshape(length, q_heads).T.reshape(rows, 1)
    mixed0 = mixed.reshape(length, q_heads, HD).transpose(1, 0, 2).reshape(rows, HD)
    which = req_prefix[0]
    rowwise = prefix_kv.reshape(block, 2 * kv_heads * HD)
    gathered = lax.all_gather(rowwise, "req", axis=0, tiled=True)
    stacked = gathered.reshape(devices, block, 2 * kv_heads * HD)
    owners = lax.dynamic_slice_in_dim(block_owner, which * owned, owned)
    pieces_out = prefix_attention(
        owners, queries.reshape(length, q_heads * HD), stacked, peak0, total0, mixed0,
        o_weight, n_tp,
    )
    summed = jnp.sum(lax.all_to_all(pieces_out, "tp", 0, 0, tiled=True).astype(jnp.float32), axis=0)
    valid = slot_index < suffix_len[0]
    return jnp.where(valid[:, None], summed, jnp.float32(0.0)).astype(jnp.bfloat16)


def solution(mesh):
    placed = (
        P("req", "tp"),
        P("tp"),
        P(None, "tp"),
        P("tp"),
        P(None, "tp"),
        P("tp"),
        P(None, "tp"),
        P("tp"),
        P("tp", None),
        P("req", None, "tp"),
        P("req"),
        P("req"),
        P(),
    )
    return jax.shard_map(
        shards, mesh=mesh, in_specs=placed, out_specs=P("req", "tp"), check_vma=False
    )
```

```python
import jax
import jax.numpy as jnp
from jax import lax
from jax.experimental import pallas as pl
from jax.experimental.pallas import tpu as pltpu
from jax.sharding import PartitionSpec as P

HD = 128
NPREF = 4


THETA = 1000000.0
EPSILON = 1e-06
ROWS = 144
PER_STEP = 4


def rotate(heads, positions):
    half = HD // 2
    freqs = THETA ** (-(jnp.arange(half, dtype=jnp.float32) * 2.0) / HD)
    angles = positions.astype(jnp.float32)[:, None] * freqs[None, :]
    cosine = jnp.cos(angles)[:, None, :]
    sine = jnp.sin(angles)[:, None, :]
    first = heads[..., :half]
    second = heads[..., half:]
    return jnp.concatenate(
        [first * cosine - second * sine, second * cosine + first * sine], axis=-1
    )


def block_stats(grouped, keys, values, allowed):
    scores = jnp.einsum(
        "sghd,kgd->sghk", grouped, keys, preferred_element_type=jnp.float32
    ) * HD ** (-0.5)
    if allowed is not None:
        scores = jnp.where(allowed[:, None, None, :], scores, -jnp.inf)
    peak = jnp.max(scores, axis=-1)
    weights = jnp.exp(scores - peak[..., None])
    total = jnp.sum(weights, axis=-1)
    mixed = jnp.einsum(
        "sghk,kgd->sghd", weights.astype(jnp.bfloat16), values, preferred_element_type=jnp.float32
    )
    return (peak, total, mixed)


def combine(first, second):
    peak = jnp.maximum(first[0], second[0])
    left = jnp.exp(first[0] - peak)
    right = jnp.exp(second[0] - peak)
    total = first[1] * left + second[1] * right
    mixed = first[2] * left[..., None] + second[2] * right[..., None]
    return (peak, total, mixed)


def prefix_kernel(own_ref, q_ref, *refs):
    kv_refs = refs[:2 * PER_STEP]
    m0_ref, l0_ref, a0_ref, w_hbm, o_ref, m_sc, l_sc, acc_sc, q_sc, w_sc, sem = refs[2 * PER_STEP:]
    step = pl.program_id(0)
    group = q_ref.shape[1] // HD
    fetch = pltpu.make_async_copy(w_hbm, w_sc, sem.at[0])

    @pl.when(step == 0)
    def _():
        fetch.start()
        m_sc[...] = m0_ref[...]
        l_sc[...] = l0_ref[...]
        acc_sc[...] = a0_ref[...]
        q = q_ref[...]
        q_sc[...] = jnp.concatenate([q[:, h * HD:(h + 1) * HD] for h in range(group)], axis=0)

    stacked = q_sc[...]
    dims = (((1,), (1,)), ((), ()))
    refs = kv_refs
    parts = [
        lax.dot_general(stacked, refs[2 * i][0], dims, preferred_element_type=jnp.float32)
        * HD ** (-0.5)
        for i in range(len(refs) // 2)
    ]
    old = m_sc[...]
    top = old
    for part in parts:
        top = jnp.maximum(top, jnp.max(part, axis=-1, keepdims=True))
    alpha = jnp.exp(old - top)
    weights = [jnp.exp(part - top) for part in parts]
    summed = weights[0].sum(axis=-1, keepdims=True)
    mixed = jnp.dot(weights[0].astype(jnp.bfloat16), refs[1][0], preferred_element_type=jnp.float32)
    for i in range(1, len(weights)):
        summed = summed + weights[i].sum(axis=-1, keepdims=True)
        mixed = mixed + jnp.dot(
            weights[i].astype(jnp.bfloat16), refs[2 * i + 1][0], preferred_element_type=jnp.float32
        )
    l_sc[...] = alpha * l_sc[...] + summed
    acc_sc[...] = alpha * acc_sc[...] + mixed
    m_sc[...] = top

    @pl.when(step == pl.num_programs(0) - 1)
    def _():
        context = (acc_sc[...] / l_sc[...]).astype(jnp.bfloat16)
        rows = q_ref.shape[0]
        flat = jnp.concatenate([context[h * rows:(h + 1) * rows] for h in range(group)], axis=1)
        fetch.wait()
        partial = jnp.dot(flat, w_sc[...], preferred_element_type=jnp.float32).astype(o_ref.dtype)
        pieces = o_ref.shape[0]
        span = o_ref.shape[2]
        for t in range(pieces):
            o_ref[t] = partial[:, t * span:(t + 1) * span]


def prefix_attention(owners, flat_q, kv, peak0, total0, mixed0, o_weight, pieces):
    length, width = flat_q.shape
    out_width = o_weight.shape[1]
    steps = owners.shape[0]
    block = kv.shape[1]
    rows = peak0.shape[0]
    cost = pl.CostEstimate(
        flops=4 * rows * block * HD * steps,
        transcendentals=rows * block * steps,
        bytes_accessed=2 * steps * block * HD * 2 + length * width * 4 + rows * HD * 4
        + width * out_width * 2 + length * out_width * 2,
    )
    return pl.pallas_call(
        prefix_kernel,
        out_shape=jax.ShapeDtypeStruct((pieces, length, out_width // pieces), jnp.bfloat16),
        grid_spec=pltpu.PrefetchScalarGridSpec(
            num_scalar_prefetch=1,
            grid=(steps // PER_STEP,),
            in_specs=[
                pl.BlockSpec((length, width), lambda j, own: (0, 0)),
                *[
                    pl.BlockSpec((1, block, HD), lambda j, own, i=i, c=c: (own[PER_STEP * j + i], 0, c))
                    for i in range(PER_STEP)
                    for c in range(2)
                ],
                pl.BlockSpec((rows, 1), lambda j, own: (0, 0)),
                pl.BlockSpec((rows, 1), lambda j, own: (0, 0)),
                pl.BlockSpec((rows, HD), lambda j, own: (0, 0)),
                pl.BlockSpec(memory_space=pl.ANY),
            ],
            out_specs=pl.BlockSpec((pieces, length, out_width // pieces), lambda j, own: (0, 0, 0)),
            scratch_shapes=[
                pltpu.VMEM((rows, 1), jnp.float32),
                pltpu.VMEM((rows, 1), jnp.float32),
                pltpu.VMEM((rows, HD), jnp.float32),
                pltpu.VMEM((rows, HD), jnp.bfloat16),
                pltpu.VMEM((width, out_width), jnp.bfloat16),
                pltpu.SemaphoreType.DMA((1,)),
            ],
        ),
        compiler_params=pltpu.CompilerParams(dimension_semantics=("arbitrary",)),
        cost_estimate=cost,
    )(owners, flat_q, *([kv] * (2 * PER_STEP)), peak0, total0, mixed0, o_weight)


def shards(
    hidden_in,
    norm_gain,
    q_weight,
    q_bias,
    k_weight,
    k_bias,
    v_weight,
    v_bias,
    o_weight,
    prefix_kv,
    suffix_len,
    req_prefix,
    block_owner,
):
    length = hidden_in.shape[0]
    devices = lax.axis_size("req")
    owned = devices // NPREF
    block = prefix_kv.shape[0]
    prefix_len = block * owned
    kv_heads = k_weight.shape[1] // HD
    q_heads = q_weight.shape[1] // HD
    group = q_heads // kv_heads
    feat = hidden_in.shape[1]
    n_tp = lax.axis_size("tp")
    packed = jnp.concatenate(
        [hidden_in, norm_gain[None, :], jnp.zeros((ROWS - length - 1, feat), hidden_in.dtype)],
        axis=0,
    )
    me_tp = lax.axis_index("tp")
    by_shift = jnp.stack(
        [packed]
        + [
            lax.ppermute(packed, "tp", [(i, (i + s) % n_tp) for i in range(n_tp)])
            for s in range(1, n_tp)
        ]
    )
    pieces_in = jnp.take(by_shift, (me_tp - jnp.arange(n_tp, dtype=jnp.int32)) % n_tp, axis=0)
    full = pieces_in.transpose(1, 0, 2).reshape(ROWS, n_tp * feat)
    tokens = full[:length].astype(jnp.float32)
    gain = full[length]
    meansq = jnp.mean(tokens * tokens, axis=-1, keepdims=True)
    normed = (tokens * lax.rsqrt(meansq + EPSILON) * gain.astype(jnp.float32)).astype(jnp.bfloat16)
    positions = prefix_len + jnp.arange(length, dtype=jnp.int32)
    queries = jnp.dot(normed, q_weight, preferred_element_type=jnp.float32) + q_bias.astype(
        jnp.float32
    )
    queries = rotate(queries.reshape(length, q_heads, HD), positions).astype(jnp.bfloat16)
    queries = queries.reshape(length, kv_heads, group, HD)
    keys = jnp.dot(normed, k_weight, preferred_element_type=jnp.float32) + k_bias.astype(
        jnp.float32
    )
    keys = rotate(keys.reshape(length, kv_heads, HD), positions).astype(jnp.bfloat16)
    values = jnp.dot(normed, v_weight, preferred_element_type=jnp.float32) + v_bias.astype(
        jnp.float32
    )
    values = values.astype(jnp.bfloat16).reshape(length, kv_heads, HD)
    slot_index = jnp.arange(length, dtype=jnp.int32)
    causal = slot_index[None, :] <= slot_index[:, None]
    peak, total, mixed = block_stats(queries, keys, values, causal)
    rows = length * q_heads
    peak0 = peak.reshape(length, q_heads).T.reshape(rows, 1)
    total0 = total.reshape(length, q_heads).T.reshape(rows, 1)
    mixed0 = mixed.reshape(length, q_heads, HD).transpose(1, 0, 2).reshape(rows, HD)
    which = req_prefix[0]
    rowwise = prefix_kv.reshape(block, 2 * kv_heads * HD)
    gathered = lax.all_gather(rowwise, "req", axis=0, tiled=True)
    stacked = gathered.reshape(devices, block, 2 * kv_heads * HD)
    owners = lax.dynamic_slice_in_dim(block_owner, which * owned, owned)
    pieces_out = prefix_attention(
        owners, queries.reshape(length, q_heads * HD), stacked, peak0, total0, mixed0,
        o_weight, n_tp,
    )
    rotated = jnp.take(pieces_out, (me_tp + jnp.arange(n_tp, dtype=jnp.int32)) % n_tp, axis=0)
    summed = rotated[0].astype(jnp.float32)
    for s in range(1, n_tp):
        summed = summed + lax.ppermute(
            rotated[s], "tp", [(i, (i + s) % n_tp) for i in range(n_tp)]
        ).astype(jnp.float32)
    valid = slot_index < suffix_len[0]
    return jnp.where(valid[:, None], summed, jnp.float32(0.0)).astype(jnp.bfloat16)


def solution(mesh):
    placed = (
        P("req", "tp"),
        P("tp"),
        P(None, "tp"),
        P("tp"),
        P(None, "tp"),
        P("tp"),
        P(None, "tp"),
        P("tp"),
        P("tp", None),
        P("req", None, "tp"),
        P("req"),
        P("req"),
        P(),
    )
    return jax.shard_map(
        shards, mesh=mesh, in_specs=placed, out_specs=P("req", "tp"), check_vma=False
    )
```

```python
import jax
import jax.numpy as jnp
from jax import lax
from jax.experimental import pallas as pl
from jax.experimental.pallas import tpu as pltpu
from jax.sharding import PartitionSpec as P

HD = 128
NPREF = 4


THETA = 1000000.0
EPSILON = 1e-06
ROWS = 144
PER_STEP = 4


def rotate(heads, positions):
    half = HD // 2
    freqs = THETA ** (-(jnp.arange(half, dtype=jnp.float32) * 2.0) / HD)
    angles = positions.astype(jnp.float32)[:, None] * freqs[None, :]
    cosine = jnp.cos(angles)[:, None, :]
    sine = jnp.sin(angles)[:, None, :]
    first = heads[..., :half]
    second = heads[..., half:]
    return jnp.concatenate(
        [first * cosine - second * sine, second * cosine + first * sine], axis=-1
    )


def block_stats(grouped, keys, values, allowed):
    scores = jnp.einsum(
        "sghd,kgd->sghk", grouped, keys, preferred_element_type=jnp.float32
    ) * HD ** (-0.5)
    if allowed is not None:
        scores = jnp.where(allowed[:, None, None, :], scores, -jnp.inf)
    peak = jnp.max(scores, axis=-1)
    weights = jnp.exp(scores - peak[..., None])
    total = jnp.sum(weights, axis=-1)
    mixed = jnp.einsum(
        "sghk,kgd->sghd", weights.astype(jnp.bfloat16), values, preferred_element_type=jnp.float32
    )
    return (peak, total, mixed)


def combine(first, second):
    peak = jnp.maximum(first[0], second[0])
    left = jnp.exp(first[0] - peak)
    right = jnp.exp(second[0] - peak)
    total = first[1] * left + second[1] * right
    mixed = first[2] * left[..., None] + second[2] * right[..., None]
    return (peak, total, mixed)


def prefix_kernel(own_ref, q_ref, *refs):
    kv_refs = refs[:2 * PER_STEP]
    m0_ref, l0_ref, a0_ref, w_hbm, o_ref, m_sc, l_sc, acc_sc, q_sc, w_sc, sem = refs[2 * PER_STEP:]
    step = pl.program_id(0)
    group = q_ref.shape[1] // HD
    fetch = pltpu.make_async_copy(w_hbm, w_sc, sem.at[0])

    @pl.when(step == 0)
    def _():
        fetch.start()
        m_sc[...] = m0_ref[...]
        l_sc[...] = l0_ref[...]
        acc_sc[...] = a0_ref[...]
        q = q_ref[...]
        q_sc[...] = jnp.concatenate([q[:, h * HD:(h + 1) * HD] for h in range(group)], axis=0)

    stacked = q_sc[...]
    dims = (((1,), (1,)), ((), ()))
    refs = kv_refs
    parts = [
        lax.dot_general(stacked, refs[2 * i][0], dims, preferred_element_type=jnp.float32)
        * HD ** (-0.5)
        for i in range(len(refs) // 2)
    ]
    old = m_sc[...]
    top = old
    for part in parts:
        top = jnp.maximum(top, jnp.max(part, axis=-1, keepdims=True))
    alpha = jnp.exp(old - top)
    weights = [jnp.exp(part - top) for part in parts]
    summed = weights[0].sum(axis=-1, keepdims=True)
    mixed = jnp.dot(weights[0].astype(jnp.bfloat16), refs[1][0], preferred_element_type=jnp.float32)
    for i in range(1, len(weights)):
        summed = summed + weights[i].sum(axis=-1, keepdims=True)
        mixed = mixed + jnp.dot(
            weights[i].astype(jnp.bfloat16), refs[2 * i + 1][0], preferred_element_type=jnp.float32
        )
    l_sc[...] = alpha * l_sc[...] + summed
    acc_sc[...] = alpha * acc_sc[...] + mixed
    m_sc[...] = top

    @pl.when(step == pl.num_programs(0) - 1)
    def _():
        context = (acc_sc[...] / l_sc[...]).astype(jnp.bfloat16)
        rows = q_ref.shape[0]
        flat = jnp.concatenate([context[h * rows:(h + 1) * rows] for h in range(group)], axis=1)
        fetch.wait()
        partial = jnp.dot(flat, w_sc[...], preferred_element_type=jnp.float32).astype(o_ref.dtype)
        pieces = o_ref.shape[0]
        span = o_ref.shape[2]
        for t in range(pieces):
            o_ref[t] = partial[:, t * span:(t + 1) * span]


def prefix_attention(owners, flat_q, kv, peak0, total0, mixed0, o_weight, pieces):
    length, width = flat_q.shape
    out_width = o_weight.shape[1]
    steps = owners.shape[0]
    block = kv.shape[1]
    rows = peak0.shape[0]
    cost = pl.CostEstimate(
        flops=4 * rows * block * HD * steps,
        transcendentals=rows * block * steps,
        bytes_accessed=2 * steps * block * HD * 2 + length * width * 4 + rows * HD * 4
        + width * out_width * 2 + length * out_width * 2,
    )
    return pl.pallas_call(
        prefix_kernel,
        out_shape=jax.ShapeDtypeStruct((pieces, length, out_width // pieces), jnp.bfloat16),
        grid_spec=pltpu.PrefetchScalarGridSpec(
            num_scalar_prefetch=1,
            grid=(steps // PER_STEP,),
            in_specs=[
                pl.BlockSpec((length, width), lambda j, own: (0, 0)),
                *[
                    pl.BlockSpec((1, block, HD), lambda j, own, i=i, c=c: (own[PER_STEP * j + i], 0, c))
                    for i in range(PER_STEP)
                    for c in range(2)
                ],
                pl.BlockSpec((rows, 1), lambda j, own: (0, 0)),
                pl.BlockSpec((rows, 1), lambda j, own: (0, 0)),
                pl.BlockSpec((rows, HD), lambda j, own: (0, 0)),
                pl.BlockSpec(memory_space=pl.ANY),
            ],
            out_specs=pl.BlockSpec((pieces, length, out_width // pieces), lambda j, own: (0, 0, 0)),
            scratch_shapes=[
                pltpu.VMEM((rows, 1), jnp.float32),
                pltpu.VMEM((rows, 1), jnp.float32),
                pltpu.VMEM((rows, HD), jnp.float32),
                pltpu.VMEM((rows, HD), jnp.bfloat16),
                pltpu.VMEM((width, out_width), jnp.bfloat16),
                pltpu.SemaphoreType.DMA((1,)),
            ],
        ),
        compiler_params=pltpu.CompilerParams(dimension_semantics=("arbitrary",)),
        cost_estimate=cost,
    )(owners, flat_q, *([kv] * (2 * PER_STEP)), peak0, total0, mixed0, o_weight)


def shards(
    hidden_in,
    norm_gain,
    q_weight,
    q_bias,
    k_weight,
    k_bias,
    v_weight,
    v_bias,
    o_weight,
    prefix_kv,
    suffix_len,
    req_prefix,
    block_owner,
):
    length = hidden_in.shape[0]
    devices = lax.axis_size("req")
    owned = devices // NPREF
    block = prefix_kv.shape[0]
    prefix_len = block * owned
    kv_heads = k_weight.shape[1] // HD
    q_heads = q_weight.shape[1] // HD
    group = q_heads // kv_heads
    feat = hidden_in.shape[1]
    n_tp = lax.axis_size("tp")
    packed = jnp.concatenate(
        [hidden_in, norm_gain[None, :], jnp.zeros((ROWS - length - 1, feat), hidden_in.dtype)],
        axis=0,
    )
    me_tp = lax.axis_index("tp")
    swapped = lax.ppermute(packed, "tp", [(i, i ^ 1) for i in range(n_tp)])
    low = me_tp % 2 == 0
    pair = jnp.stack([jnp.where(low, packed, swapped), jnp.where(low, swapped, packed)])
    n_x = n_tp // 2
    along = jnp.stack(
        [pair]
        + [
            lax.ppermute(pair, "tp", [(i, (i + 2 * u) % n_tp) for i in range(n_tp)])
            for u in range(1, n_x)
        ]
    )
    me_x = me_tp // 2
    ordered = jnp.take(along, (me_x - jnp.arange(n_x, dtype=jnp.int32)) % n_x, axis=0)
    pieces_in = ordered.reshape((n_tp,) + packed.shape)
    full = pieces_in.transpose(1, 0, 2).reshape(ROWS, n_tp * feat)
    tokens = full[:length].astype(jnp.float32)
    gain = full[length]
    meansq = jnp.mean(tokens * tokens, axis=-1, keepdims=True)
    normed = (tokens * lax.rsqrt(meansq + EPSILON) * gain.astype(jnp.float32)).astype(jnp.bfloat16)
    positions = prefix_len + jnp.arange(length, dtype=jnp.int32)
    queries = jnp.dot(normed, q_weight, preferred_element_type=jnp.float32) + q_bias.astype(
        jnp.float32
    )
    queries = rotate(queries.reshape(length, q_heads, HD), positions).astype(jnp.bfloat16)
    queries = queries.reshape(length, kv_heads, group, HD)
    keys = jnp.dot(normed, k_weight, preferred_element_type=jnp.float32) + k_bias.astype(
        jnp.float32
    )
    keys = rotate(keys.reshape(length, kv_heads, HD), positions).astype(jnp.bfloat16)
    values = jnp.dot(normed, v_weight, preferred_element_type=jnp.float32) + v_bias.astype(
        jnp.float32
    )
    values = values.astype(jnp.bfloat16).reshape(length, kv_heads, HD)
    slot_index = jnp.arange(length, dtype=jnp.int32)
    causal = slot_index[None, :] <= slot_index[:, None]
    peak, total, mixed = block_stats(queries, keys, values, causal)
    rows = length * q_heads
    peak0 = peak.reshape(length, q_heads).T.reshape(rows, 1)
    total0 = total.reshape(length, q_heads).T.reshape(rows, 1)
    mixed0 = mixed.reshape(length, q_heads, HD).transpose(1, 0, 2).reshape(rows, HD)
    which = req_prefix[0]
    rowwise = prefix_kv.reshape(block, 2 * kv_heads * HD)
    gathered = lax.all_gather(rowwise, "req", axis=0, tiled=True)
    stacked = gathered.reshape(devices, block, 2 * kv_heads * HD)
    owners = lax.dynamic_slice_in_dim(block_owner, which * owned, owned)
    pieces_out = prefix_attention(
        owners, queries.reshape(length, q_heads * HD), stacked, peak0, total0, mixed0,
        o_weight, n_tp,
    )
    summed = jnp.sum(lax.all_to_all(pieces_out, "tp", 0, 0, tiled=True).astype(jnp.float32), axis=0)
    valid = slot_index < suffix_len[0]
    return jnp.where(valid[:, None], summed, jnp.float32(0.0)).astype(jnp.bfloat16)


def solution(mesh):
    placed = (
        P("req", "tp"),
        P("tp"),
        P(None, "tp"),
        P("tp"),
        P(None, "tp"),
        P("tp"),
        P(None, "tp"),
        P("tp"),
        P("tp", None),
        P("req", None, "tp"),
        P("req"),
        P("req"),
        P(),
    )
    return jax.shard_map(
        shards, mesh=mesh, in_specs=placed, out_specs=P("req", "tp"), check_vma=False
    )
```

```python
import jax
import jax.numpy as jnp
from jax import lax
from jax.experimental import pallas as pl
from jax.experimental.pallas import tpu as pltpu
from jax.sharding import PartitionSpec as P

HD = 128
NPREF = 4


THETA = 1000000.0
EPSILON = 1e-06
ROWS = 144
PER_STEP = 8


def rotate(heads, positions):
    half = HD // 2
    freqs = THETA ** (-(jnp.arange(half, dtype=jnp.float32) * 2.0) / HD)
    angles = positions.astype(jnp.float32)[:, None] * freqs[None, :]
    cosine = jnp.cos(angles)[:, None, :]
    sine = jnp.sin(angles)[:, None, :]
    first = heads[..., :half]
    second = heads[..., half:]
    return jnp.concatenate(
        [first * cosine - second * sine, second * cosine + first * sine], axis=-1
    )


def block_stats(grouped, keys, values, allowed):
    scores = jnp.einsum(
        "sghd,kgd->sghk", grouped, keys, preferred_element_type=jnp.float32
    ) * HD ** (-0.5)
    if allowed is not None:
        scores = jnp.where(allowed[:, None, None, :], scores, -jnp.inf)
    peak = jnp.max(scores, axis=-1)
    weights = jnp.exp(scores - peak[..., None])
    total = jnp.sum(weights, axis=-1)
    mixed = jnp.einsum(
        "sghk,kgd->sghd", weights.astype(jnp.bfloat16), values, preferred_element_type=jnp.float32
    )
    return (peak, total, mixed)


def combine(first, second):
    peak = jnp.maximum(first[0], second[0])
    left = jnp.exp(first[0] - peak)
    right = jnp.exp(second[0] - peak)
    total = first[1] * left + second[1] * right
    mixed = first[2] * left[..., None] + second[2] * right[..., None]
    return (peak, total, mixed)


def prefix_kernel(own_ref, q_ref, *refs):
    kv_refs = refs[:2 * PER_STEP]
    m0_ref, l0_ref, a0_ref, w_hbm, o_ref, m_sc, l_sc, acc_sc, q_sc, w_sc, sem = refs[2 * PER_STEP:]
    step = pl.program_id(0)
    group = q_ref.shape[1] // HD
    fetch = pltpu.make_async_copy(w_hbm, w_sc, sem.at[0])

    @pl.when(step == 0)
    def _():
        fetch.start()
        m_sc[...] = m0_ref[...]
        l_sc[...] = l0_ref[...]
        acc_sc[...] = a0_ref[...]
        q = q_ref[...]
        q_sc[...] = jnp.concatenate([q[:, h * HD:(h + 1) * HD] for h in range(group)], axis=0)

    stacked = q_sc[...]
    dims = (((1,), (1,)), ((), ()))
    refs = kv_refs
    parts = [
        lax.dot_general(stacked, refs[2 * i][0], dims, preferred_element_type=jnp.float32)
        * HD ** (-0.5)
        for i in range(len(refs) // 2)
    ]
    old = m_sc[...]
    top = old
    for part in parts:
        top = jnp.maximum(top, jnp.max(part, axis=-1, keepdims=True))
    alpha = jnp.exp(old - top)
    weights = [jnp.exp(part - top) for part in parts]
    summed = weights[0].sum(axis=-1, keepdims=True)
    mixed = jnp.dot(weights[0].astype(jnp.bfloat16), refs[1][0], preferred_element_type=jnp.float32)
    for i in range(1, len(weights)):
        summed = summed + weights[i].sum(axis=-1, keepdims=True)
        mixed = mixed + jnp.dot(
            weights[i].astype(jnp.bfloat16), refs[2 * i + 1][0], preferred_element_type=jnp.float32
        )
    l_sc[...] = alpha * l_sc[...] + summed
    acc_sc[...] = alpha * acc_sc[...] + mixed
    m_sc[...] = top

    @pl.when(step == pl.num_programs(0) - 1)
    def _():
        context = (acc_sc[...] / l_sc[...]).astype(jnp.bfloat16)
        rows = q_ref.shape[0]
        flat = jnp.concatenate([context[h * rows:(h + 1) * rows] for h in range(group)], axis=1)
        fetch.wait()
        partial = jnp.dot(flat, w_sc[...], preferred_element_type=jnp.float32).astype(o_ref.dtype)
        pieces = o_ref.shape[0]
        span = o_ref.shape[2]
        for t in range(pieces):
            o_ref[t] = partial[:, t * span:(t + 1) * span]


def prefix_attention(owners, flat_q, kv, peak0, total0, mixed0, o_weight, pieces):
    length, width = flat_q.shape
    out_width = o_weight.shape[1]
    steps = owners.shape[0]
    block = kv.shape[1]
    rows = peak0.shape[0]
    cost = pl.CostEstimate(
        flops=4 * rows * block * HD * steps,
        transcendentals=rows * block * steps,
        bytes_accessed=2 * steps * block * HD * 2 + length * width * 4 + rows * HD * 4
        + width * out_width * 2 + length * out_width * 2,
    )
    return pl.pallas_call(
        prefix_kernel,
        out_shape=jax.ShapeDtypeStruct((pieces, length, out_width // pieces), jnp.bfloat16),
        grid_spec=pltpu.PrefetchScalarGridSpec(
            num_scalar_prefetch=1,
            grid=(steps // PER_STEP,),
            in_specs=[
                pl.BlockSpec((length, width), lambda j, own: (0, 0)),
                *[
                    pl.BlockSpec((1, block, HD), lambda j, own, i=i, c=c: (own[PER_STEP * j + i], 0, c))
                    for i in range(PER_STEP)
                    for c in range(2)
                ],
                pl.BlockSpec((rows, 1), lambda j, own: (0, 0)),
                pl.BlockSpec((rows, 1), lambda j, own: (0, 0)),
                pl.BlockSpec((rows, HD), lambda j, own: (0, 0)),
                pl.BlockSpec(memory_space=pl.ANY),
            ],
            out_specs=pl.BlockSpec((pieces, length, out_width // pieces), lambda j, own: (0, 0, 0)),
            scratch_shapes=[
                pltpu.VMEM((rows, 1), jnp.float32),
                pltpu.VMEM((rows, 1), jnp.float32),
                pltpu.VMEM((rows, HD), jnp.float32),
                pltpu.VMEM((rows, HD), jnp.bfloat16),
                pltpu.VMEM((width, out_width), jnp.bfloat16),
                pltpu.SemaphoreType.DMA((1,)),
            ],
        ),
        compiler_params=pltpu.CompilerParams(dimension_semantics=("arbitrary",)),
        cost_estimate=cost,
    )(owners, flat_q, *([kv] * (2 * PER_STEP)), peak0, total0, mixed0, o_weight)


def shards(
    hidden_in,
    norm_gain,
    q_weight,
    q_bias,
    k_weight,
    k_bias,
    v_weight,
    v_bias,
    o_weight,
    prefix_kv,
    suffix_len,
    req_prefix,
    block_owner,
):
    length = hidden_in.shape[0]
    devices = lax.axis_size("req")
    owned = devices // NPREF
    block = prefix_kv.shape[0]
    prefix_len = block * owned
    kv_heads = k_weight.shape[1] // HD
    q_heads = q_weight.shape[1] // HD
    group = q_heads // kv_heads
    feat = hidden_in.shape[1]
    n_tp = lax.axis_size("tp")
    packed = jnp.concatenate(
        [hidden_in, norm_gain[None, :], jnp.zeros((ROWS - length - 1, feat), hidden_in.dtype)],
        axis=0,
    )
    me_tp = lax.axis_index("tp")
    swapped = lax.ppermute(packed, "tp", [(i, i ^ 1) for i in range(n_tp)])
    low = me_tp % 2 == 0
    pair = jnp.stack([jnp.where(low, packed, swapped), jnp.where(low, swapped, packed)])
    n_x = n_tp // 2
    along = jnp.stack(
        [pair]
        + [
            lax.ppermute(pair, "tp", [(i, (i + 2 * u) % n_tp) for i in range(n_tp)])
            for u in range(1, n_x)
        ]
    )
    me_x = me_tp // 2
    ordered = jnp.take(along, (me_x - jnp.arange(n_x, dtype=jnp.int32)) % n_x, axis=0)
    pieces_in = ordered.reshape((n_tp,) + packed.shape)
    full = pieces_in.transpose(1, 0, 2).reshape(ROWS, n_tp * feat)
    tokens = full[:length].astype(jnp.float32)
    gain = full[length]
    meansq = jnp.mean(tokens * tokens, axis=-1, keepdims=True)
    normed = (tokens * lax.rsqrt(meansq + EPSILON) * gain.astype(jnp.float32)).astype(jnp.bfloat16)
    positions = prefix_len + jnp.arange(length, dtype=jnp.int32)
    queries = jnp.dot(normed, q_weight, preferred_element_type=jnp.float32) + q_bias.astype(
        jnp.float32
    )
    queries = rotate(queries.reshape(length, q_heads, HD), positions).astype(jnp.bfloat16)
    queries = queries.reshape(length, kv_heads, group, HD)
    keys = jnp.dot(normed, k_weight, preferred_element_type=jnp.float32) + k_bias.astype(
        jnp.float32
    )
    keys = rotate(keys.reshape(length, kv_heads, HD), positions).astype(jnp.bfloat16)
    values = jnp.dot(normed, v_weight, preferred_element_type=jnp.float32) + v_bias.astype(
        jnp.float32
    )
    values = values.astype(jnp.bfloat16).reshape(length, kv_heads, HD)
    slot_index = jnp.arange(length, dtype=jnp.int32)
    causal = slot_index[None, :] <= slot_index[:, None]
    peak, total, mixed = block_stats(queries, keys, values, causal)
    rows = length * q_heads
    peak0 = peak.reshape(length, q_heads).T.reshape(rows, 1)
    total0 = total.reshape(length, q_heads).T.reshape(rows, 1)
    mixed0 = mixed.reshape(length, q_heads, HD).transpose(1, 0, 2).reshape(rows, HD)
    which = req_prefix[0]
    rowwise = prefix_kv.reshape(block, 2 * kv_heads * HD)
    gathered = lax.all_gather(rowwise, "req", axis=0, tiled=True)
    stacked = gathered.reshape(devices, block, 2 * kv_heads * HD)
    owners = lax.dynamic_slice_in_dim(block_owner, which * owned, owned)
    pieces_out = prefix_attention(
        owners, queries.reshape(length, q_heads * HD), stacked, peak0, total0, mixed0,
        o_weight, n_tp,
    )
    summed = jnp.sum(lax.all_to_all(pieces_out, "tp", 0, 0, tiled=True).astype(jnp.float32), axis=0)
    valid = slot_index < suffix_len[0]
    return jnp.where(valid[:, None], summed, jnp.float32(0.0)).astype(jnp.bfloat16)


def solution(mesh):
    placed = (
        P("req", "tp"),
        P("tp"),
        P(None, "tp"),
        P("tp"),
        P(None, "tp"),
        P("tp"),
        P(None, "tp"),
        P("tp"),
        P("tp", None),
        P("req", None, "tp"),
        P("req"),
        P("req"),
        P(),
    )
    return jax.shard_map(
        shards, mesh=mesh, in_specs=placed, out_specs=P("req", "tp"), check_vma=False
    )
```

```python
import jax
import jax.numpy as jnp
from jax import lax
from jax.experimental import pallas as pl
from jax.experimental.pallas import tpu as pltpu
from jax.sharding import PartitionSpec as P

HD = 128
NPREF = 4


THETA = 1000000.0
EPSILON = 1e-06
ROWS = 144
PER_STEP = 8


def rotate(heads, positions):
    half = HD // 2
    freqs = THETA ** (-(jnp.arange(half, dtype=jnp.float32) * 2.0) / HD)
    angles = positions.astype(jnp.float32)[:, None] * freqs[None, :]
    cosine = jnp.cos(angles)[:, None, :]
    sine = jnp.sin(angles)[:, None, :]
    first = heads[..., :half]
    second = heads[..., half:]
    return jnp.concatenate(
        [first * cosine - second * sine, second * cosine + first * sine], axis=-1
    )


def block_stats(grouped, keys, values, allowed):
    scores = jnp.einsum(
        "sghd,kgd->sghk", grouped, keys, preferred_element_type=jnp.float32
    ) * HD ** (-0.5)
    if allowed is not None:
        scores = jnp.where(allowed[:, None, None, :], scores, -jnp.inf)
    peak = jnp.max(scores, axis=-1)
    weights = jnp.exp(scores - peak[..., None])
    total = jnp.sum(weights, axis=-1)
    mixed = jnp.einsum(
        "sghk,kgd->sghd", weights.astype(jnp.bfloat16), values, preferred_element_type=jnp.float32
    )
    return (peak, total, mixed)


def combine(first, second):
    peak = jnp.maximum(first[0], second[0])
    left = jnp.exp(first[0] - peak)
    right = jnp.exp(second[0] - peak)
    total = first[1] * left + second[1] * right
    mixed = first[2] * left[..., None] + second[2] * right[..., None]
    return (peak, total, mixed)


def prefix_kernel(own_ref, q_ref, kv_hbm, m0_ref, l0_ref, a0_ref, w_hbm, o_ref, buf, w_sc, sem):
    group = q_ref.shape[1] // HD
    steps = buf.shape[0]
    fetch = pltpu.make_async_copy(w_hbm, w_sc, sem.at[steps])
    copies = [
        pltpu.make_async_copy(kv_hbm.at[own_ref[i]], buf.at[i], sem.at[i]) for i in range(steps)
    ]
    for copy in copies:
        copy.start()
    fetch.start()
    q = q_ref[...]
    stacked = jnp.concatenate([q[:, h * HD:(h + 1) * HD] for h in range(group)], axis=0)
    dims = (((1,), (1,)), ((), ()))
    top = m0_ref[...]
    summed = l0_ref[...]
    mixed = a0_ref[...]
    for i in range(steps):
        copies[i].wait()
        keys = buf[i, :, :HD]
        values = buf[i, :, HD:]
        part = lax.dot_general(stacked, keys, dims, preferred_element_type=jnp.float32) * HD ** (-0.5)
        new = jnp.maximum(top, jnp.max(part, axis=-1, keepdims=True))
        alpha = jnp.exp(top - new)
        weights = jnp.exp(part - new)
        summed = alpha * summed + weights.sum(axis=-1, keepdims=True)
        mixed = alpha * mixed + jnp.dot(
            weights.astype(jnp.bfloat16), values, preferred_element_type=jnp.float32
        )
        top = new
    context = (mixed / summed).astype(jnp.bfloat16)
    rows = q_ref.shape[0]
    flat = jnp.concatenate([context[h * rows:(h + 1) * rows] for h in range(group)], axis=1)
    fetch.wait()
    partial = jnp.dot(flat, w_sc[...], preferred_element_type=jnp.float32).astype(o_ref.dtype)
    pieces = o_ref.shape[0]
    span = o_ref.shape[2]
    for t in range(pieces):
        o_ref[t] = partial[:, t * span:(t + 1) * span]


def prefix_attention(owners, flat_q, kv, peak0, total0, mixed0, o_weight, pieces):
    length, width = flat_q.shape
    out_width = o_weight.shape[1]
    steps = owners.shape[0]
    block = kv.shape[1]
    rows = peak0.shape[0]
    cost = pl.CostEstimate(
        flops=4 * rows * block * HD * steps,
        transcendentals=rows * block * steps,
        bytes_accessed=2 * steps * block * HD * 2 + length * width * 4 + rows * HD * 4
        + width * out_width * 2 + length * out_width * 2,
    )
    return pl.pallas_call(
        prefix_kernel,
        out_shape=jax.ShapeDtypeStruct((pieces, length, out_width // pieces), jnp.bfloat16),
        grid_spec=pltpu.PrefetchScalarGridSpec(
            num_scalar_prefetch=1,
            grid=(1,),
            in_specs=[
                pl.BlockSpec((length, width), lambda j, own: (0, 0)),
                pl.BlockSpec(memory_space=pl.ANY),
                pl.BlockSpec((rows, 1), lambda j, own: (0, 0)),
                pl.BlockSpec((rows, 1), lambda j, own: (0, 0)),
                pl.BlockSpec((rows, HD), lambda j, own: (0, 0)),
                pl.BlockSpec(memory_space=pl.ANY),
            ],
            out_specs=pl.BlockSpec((pieces, length, out_width // pieces), lambda j, own: (0, 0, 0)),
            scratch_shapes=[
                pltpu.VMEM((steps, block, 2 * HD), jnp.bfloat16),
                pltpu.VMEM((width, out_width), jnp.bfloat16),
                pltpu.SemaphoreType.DMA((steps + 1,)),
            ],
        ),
        compiler_params=pltpu.CompilerParams(dimension_semantics=("arbitrary",)),
        cost_estimate=cost,
    )(owners, flat_q, kv, peak0, total0, mixed0, o_weight)


def shards(
    hidden_in,
    norm_gain,
    q_weight,
    q_bias,
    k_weight,
    k_bias,
    v_weight,
    v_bias,
    o_weight,
    prefix_kv,
    suffix_len,
    req_prefix,
    block_owner,
):
    length = hidden_in.shape[0]
    devices = lax.axis_size("req")
    owned = devices // NPREF
    block = prefix_kv.shape[0]
    prefix_len = block * owned
    kv_heads = k_weight.shape[1] // HD
    q_heads = q_weight.shape[1] // HD
    group = q_heads // kv_heads
    feat = hidden_in.shape[1]
    n_tp = lax.axis_size("tp")
    packed = jnp.concatenate(
        [hidden_in, norm_gain[None, :], jnp.zeros((ROWS - length - 1, feat), hidden_in.dtype)],
        axis=0,
    )
    me_tp = lax.axis_index("tp")
    swapped = lax.ppermute(packed, "tp", [(i, i ^ 1) for i in range(n_tp)])
    low = me_tp % 2 == 0
    pair = jnp.stack([jnp.where(low, packed, swapped), jnp.where(low, swapped, packed)])
    n_x = n_tp // 2
    along = jnp.stack(
        [pair]
        + [
            lax.ppermute(pair, "tp", [(i, (i + 2 * u) % n_tp) for i in range(n_tp)])
            for u in range(1, n_x)
        ]
    )
    me_x = me_tp // 2
    ordered = jnp.take(along, (me_x - jnp.arange(n_x, dtype=jnp.int32)) % n_x, axis=0)
    pieces_in = ordered.reshape((n_tp,) + packed.shape)
    full = pieces_in.transpose(1, 0, 2).reshape(ROWS, n_tp * feat)
    tokens = full[:length].astype(jnp.float32)
    gain = full[length]
    meansq = jnp.mean(tokens * tokens, axis=-1, keepdims=True)
    normed = (tokens * lax.rsqrt(meansq + EPSILON) * gain.astype(jnp.float32)).astype(jnp.bfloat16)
    positions = prefix_len + jnp.arange(length, dtype=jnp.int32)
    queries = jnp.dot(normed, q_weight, preferred_element_type=jnp.float32) + q_bias.astype(
        jnp.float32
    )
    queries = rotate(queries.reshape(length, q_heads, HD), positions).astype(jnp.bfloat16)
    queries = queries.reshape(length, kv_heads, group, HD)
    keys = jnp.dot(normed, k_weight, preferred_element_type=jnp.float32) + k_bias.astype(
        jnp.float32
    )
    keys = rotate(keys.reshape(length, kv_heads, HD), positions).astype(jnp.bfloat16)
    values = jnp.dot(normed, v_weight, preferred_element_type=jnp.float32) + v_bias.astype(
        jnp.float32
    )
    values = values.astype(jnp.bfloat16).reshape(length, kv_heads, HD)
    slot_index = jnp.arange(length, dtype=jnp.int32)
    causal = slot_index[None, :] <= slot_index[:, None]
    peak, total, mixed = block_stats(queries, keys, values, causal)
    rows = length * q_heads
    peak0 = peak.reshape(length, q_heads).T.reshape(rows, 1)
    total0 = total.reshape(length, q_heads).T.reshape(rows, 1)
    mixed0 = mixed.reshape(length, q_heads, HD).transpose(1, 0, 2).reshape(rows, HD)
    which = req_prefix[0]
    rowwise = prefix_kv.reshape(block, 2 * kv_heads * HD)
    gathered = lax.all_gather(rowwise, "req", axis=0, tiled=True)
    stacked = gathered.reshape(devices, block, 2 * kv_heads * HD)
    owners = lax.dynamic_slice_in_dim(block_owner, which * owned, owned)
    pieces_out = prefix_attention(
        owners, queries.reshape(length, q_heads * HD), stacked, peak0, total0, mixed0,
        o_weight, n_tp,
    )
    summed = jnp.sum(lax.all_to_all(pieces_out, "tp", 0, 0, tiled=True).astype(jnp.float32), axis=0)
    valid = slot_index < suffix_len[0]
    return jnp.where(valid[:, None], summed, jnp.float32(0.0)).astype(jnp.bfloat16)


def solution(mesh):
    placed = (
        P("req", "tp"),
        P("tp"),
        P(None, "tp"),
        P("tp"),
        P(None, "tp"),
        P("tp"),
        P(None, "tp"),
        P("tp"),
        P("tp", None),
        P("req", None, "tp"),
        P("req"),
        P("req"),
        P(),
    )
    return jax.shard_map(
        shards, mesh=mesh, in_specs=placed, out_specs=P("req", "tp"), check_vma=False
    )
```

```python
import jax
import jax.numpy as jnp
from jax import lax
from jax.experimental import pallas as pl
from jax.experimental.pallas import tpu as pltpu
from jax.sharding import PartitionSpec as P

HD = 128
NPREF = 4


THETA = 1000000.0
EPSILON = 1e-06
ROWS = 144
PER_STEP = 8


def rotate(heads, positions):
    half = HD // 2
    freqs = THETA ** (-(jnp.arange(half, dtype=jnp.float32) * 2.0) / HD)
    angles = positions.astype(jnp.float32)[:, None] * freqs[None, :]
    cosine = jnp.cos(angles)[:, None, :]
    sine = jnp.sin(angles)[:, None, :]
    first = heads[..., :half]
    second = heads[..., half:]
    return jnp.concatenate(
        [first * cosine - second * sine, second * cosine + first * sine], axis=-1
    )


def block_stats(grouped, keys, values, allowed):
    scores = jnp.einsum(
        "sghd,kgd->sghk", grouped, keys, preferred_element_type=jnp.float32
    ) * HD ** (-0.5)
    if allowed is not None:
        scores = jnp.where(allowed[:, None, None, :], scores, -jnp.inf)
    peak = jnp.max(scores, axis=-1)
    weights = jnp.exp(scores - peak[..., None])
    total = jnp.sum(weights, axis=-1)
    mixed = jnp.einsum(
        "sghk,kgd->sghd", weights.astype(jnp.bfloat16), values, preferred_element_type=jnp.float32
    )
    return (peak, total, mixed)


def combine(first, second):
    peak = jnp.maximum(first[0], second[0])
    left = jnp.exp(first[0] - peak)
    right = jnp.exp(second[0] - peak)
    total = first[1] * left + second[1] * right
    mixed = first[2] * left[..., None] + second[2] * right[..., None]
    return (peak, total, mixed)


def prefix_kernel(own_ref, q_ref, *refs):
    kv_refs = refs[:2 * PER_STEP]
    m0_ref, l0_ref, a0_ref, w_hbm, o_ref, w_sc, sem = refs[2 * PER_STEP:]
    group = q_ref.shape[1] // HD
    fetch = pltpu.make_async_copy(w_hbm, w_sc, sem.at[0])
    fetch.start()
    q = q_ref[...]
    stacked = jnp.concatenate([q[:, h * HD:(h + 1) * HD] for h in range(group)], axis=0)
    dims = (((1,), (1,)), ((), ()))
    parts = [
        lax.dot_general(stacked, kv_refs[2 * i][0], dims, preferred_element_type=jnp.float32)
        * HD ** (-0.5)
        for i in range(PER_STEP)
    ]
    old = m0_ref[...]
    top = old
    for part in parts:
        top = jnp.maximum(top, jnp.max(part, axis=-1, keepdims=True))
    alpha = jnp.exp(old - top)
    weights = [jnp.exp(part - top) for part in parts]
    summed = weights[0].sum(axis=-1, keepdims=True)
    mixed = jnp.dot(weights[0].astype(jnp.bfloat16), kv_refs[1][0], preferred_element_type=jnp.float32)
    for i in range(1, PER_STEP):
        summed = summed + weights[i].sum(axis=-1, keepdims=True)
        mixed = mixed + jnp.dot(
            weights[i].astype(jnp.bfloat16), kv_refs[2 * i + 1][0], preferred_element_type=jnp.float32
        )
    total = alpha * l0_ref[...] + summed
    acc = alpha * a0_ref[...] + mixed
    context = (acc / total).astype(jnp.bfloat16)
    rows = q_ref.shape[0]
    flat = jnp.concatenate([context[h * rows:(h + 1) * rows] for h in range(group)], axis=1)
    fetch.wait()
    partial = jnp.dot(flat, w_sc[...], preferred_element_type=jnp.float32).astype(o_ref.dtype)
    pieces = o_ref.shape[0]
    span = o_ref.shape[2]
    for t in range(pieces):
        o_ref[t] = partial[:, t * span:(t + 1) * span]


def prefix_attention(owners, flat_q, kv, peak0, total0, mixed0, o_weight, pieces):
    length, width = flat_q.shape
    out_width = o_weight.shape[1]
    steps = owners.shape[0]
    block = kv.shape[1]
    rows = peak0.shape[0]
    cost = pl.CostEstimate(
        flops=4 * rows * block * HD * steps,
        transcendentals=rows * block * steps,
        bytes_accessed=2 * steps * block * HD * 2 + length * width * 4 + rows * HD * 4
        + width * out_width * 2 + length * out_width * 2,
    )
    return pl.pallas_call(
        prefix_kernel,
        out_shape=jax.ShapeDtypeStruct((pieces, length, out_width // pieces), jnp.bfloat16),
        grid_spec=pltpu.PrefetchScalarGridSpec(
            num_scalar_prefetch=1,
            grid=(steps // PER_STEP,),
            in_specs=[
                pl.BlockSpec((length, width), lambda j, own: (0, 0)),
                *[
                    pl.BlockSpec((1, block, HD), lambda j, own, i=i, c=c: (own[PER_STEP * j + i], 0, c))
                    for i in range(PER_STEP)
                    for c in range(2)
                ],
                pl.BlockSpec((rows, 1), lambda j, own: (0, 0)),
                pl.BlockSpec((rows, 1), lambda j, own: (0, 0)),
                pl.BlockSpec((rows, HD), lambda j, own: (0, 0)),
                pl.BlockSpec(memory_space=pl.ANY),
            ],
            out_specs=pl.BlockSpec((pieces, length, out_width // pieces), lambda j, own: (0, 0, 0)),
            scratch_shapes=[
                pltpu.VMEM((width, out_width), jnp.bfloat16),
                pltpu.SemaphoreType.DMA((1,)),
            ],
        ),
        compiler_params=pltpu.CompilerParams(dimension_semantics=("arbitrary",)),
        cost_estimate=cost,
    )(owners, flat_q, *([kv] * (2 * PER_STEP)), peak0, total0, mixed0, o_weight)


def shards(
    hidden_in,
    norm_gain,
    q_weight,
    q_bias,
    k_weight,
    k_bias,
    v_weight,
    v_bias,
    o_weight,
    prefix_kv,
    suffix_len,
    req_prefix,
    block_owner,
):
    length = hidden_in.shape[0]
    devices = lax.axis_size("req")
    owned = devices // NPREF
    block = prefix_kv.shape[0]
    prefix_len = block * owned
    kv_heads = k_weight.shape[1] // HD
    q_heads = q_weight.shape[1] // HD
    group = q_heads // kv_heads
    feat = hidden_in.shape[1]
    n_tp = lax.axis_size("tp")
    packed = jnp.concatenate(
        [hidden_in, norm_gain[None, :], jnp.zeros((ROWS - length - 1, feat), hidden_in.dtype)],
        axis=0,
    )
    me_tp = lax.axis_index("tp")
    swapped = lax.ppermute(packed, "tp", [(i, i ^ 1) for i in range(n_tp)])
    low = me_tp % 2 == 0
    pair = jnp.stack([jnp.where(low, packed, swapped), jnp.where(low, swapped, packed)])
    n_x = n_tp // 2
    along = jnp.stack(
        [pair]
        + [
            lax.ppermute(pair, "tp", [(i, (i + 2 * u) % n_tp) for i in range(n_tp)])
            for u in range(1, n_x)
        ]
    )
    me_x = me_tp // 2
    ordered = jnp.take(along, (me_x - jnp.arange(n_x, dtype=jnp.int32)) % n_x, axis=0)
    pieces_in = ordered.reshape((n_tp,) + packed.shape)
    full = pieces_in.transpose(1, 0, 2).reshape(ROWS, n_tp * feat)
    tokens = full[:length].astype(jnp.float32)
    gain = full[length]
    meansq = jnp.mean(tokens * tokens, axis=-1, keepdims=True)
    normed = (tokens * lax.rsqrt(meansq + EPSILON) * gain.astype(jnp.float32)).astype(jnp.bfloat16)
    positions = prefix_len + jnp.arange(length, dtype=jnp.int32)
    queries = jnp.dot(normed, q_weight, preferred_element_type=jnp.float32) + q_bias.astype(
        jnp.float32
    )
    queries = rotate(queries.reshape(length, q_heads, HD), positions).astype(jnp.bfloat16)
    queries = queries.reshape(length, kv_heads, group, HD)
    keys = jnp.dot(normed, k_weight, preferred_element_type=jnp.float32) + k_bias.astype(
        jnp.float32
    )
    keys = rotate(keys.reshape(length, kv_heads, HD), positions).astype(jnp.bfloat16)
    values = jnp.dot(normed, v_weight, preferred_element_type=jnp.float32) + v_bias.astype(
        jnp.float32
    )
    values = values.astype(jnp.bfloat16).reshape(length, kv_heads, HD)
    slot_index = jnp.arange(length, dtype=jnp.int32)
    causal = slot_index[None, :] <= slot_index[:, None]
    peak, total, mixed = block_stats(queries, keys, values, causal)
    rows = length * q_heads
    peak0 = peak.reshape(length, q_heads).T.reshape(rows, 1)
    total0 = total.reshape(length, q_heads).T.reshape(rows, 1)
    mixed0 = mixed.reshape(length, q_heads, HD).transpose(1, 0, 2).reshape(rows, HD)
    which = req_prefix[0]
    rowwise = prefix_kv.reshape(block, 2 * kv_heads * HD)
    gathered = lax.all_gather(rowwise, "req", axis=0, tiled=True)
    stacked = gathered.reshape(devices, block, 2 * kv_heads * HD)
    owners = lax.dynamic_slice_in_dim(block_owner, which * owned, owned)
    pieces_out = prefix_attention(
        owners, queries.reshape(length, q_heads * HD), stacked, peak0, total0, mixed0,
        o_weight, n_tp,
    )
    summed = jnp.sum(lax.all_to_all(pieces_out, "tp", 0, 0, tiled=True).astype(jnp.float32), axis=0)
    valid = slot_index < suffix_len[0]
    return jnp.where(valid[:, None], summed, jnp.float32(0.0)).astype(jnp.bfloat16)


def solution(mesh):
    placed = (
        P("req", "tp"),
        P("tp"),
        P(None, "tp"),
        P("tp"),
        P(None, "tp"),
        P("tp"),
        P(None, "tp"),
        P("tp"),
        P("tp", None),
        P("req", None, "tp"),
        P("req"),
        P("req"),
        P(),
    )
    return jax.shard_map(
        shards, mesh=mesh, in_specs=placed, out_specs=P("req", "tp"), check_vma=False
    )
```
